256 devices in a mesh: tok: 64 (over z, y, core), pool: 4 (over x).
Axes of the slice: x: 4, y: 4, z: 8, core: 2. Of those that a mesh axis runs over, the one named last changes fastest.
Arguments:
- stream: bfloat16 [16384, 1024], P(('tok', 'pool')), may hold values from -6 to 6
- queries: bfloat16 [16384, 1024], P(('tok', 'pool')), may hold values from -2000 to 2000
- fresh_kv: bfloat16 [16384, 1024], P(('tok', 'pool')), may hold values from -16 to 16
- cache_block_pool: bfloat16 [2048, 64, 1024], P(('tok', 'pool')), may hold values from -9 to 9
- block_table: int32 [64, 16], P('tok'), may hold values from 0 to 31, as said below
- cached_len: int32 [64, 3], P('tok'), may hold values from 1 to 1024, as said below
- request_ids: int32 [64, 256], P('tok'), may hold values from 0 to 2, never falling along the last dimension, each value on 1 to 128 neighbouring positions
- output_weight: bfloat16 [1024, 1024], replicated, may hold values from -0.1875 to 0.1875
- norm_gain: float32 [1024], replicated, may hold values from 0.5 to 1.5
- expert_gate_up: bfloat16 [64, 1024, 512], P('tok'), may hold values from -0.1875 to 0.1875
- expert_down: bfloat16 [64, 256, 1024], P('tok'), may hold values from -0.25 to 0.25
- routes: int32 [16384, 8], P(('tok', 'pool')), may hold values from 0 to 31, all different within a row; in each aligned block of 64 rows (0 to 63, 64 to 127, ...) at most 32 rows name the same one
- route_weight: float32 [16384, 8], P(('tok', 'pool')), may hold values from 0.05 to 0.4
Outputs:
- attended: bfloat16 [16384, 1024], P(('tok', 'pool'))
- layer_out: bfloat16 [16384, 1024], P(('tok', 'pool'))
The draws below stay inside these ranges and needn't reach their ends.
Inputs may be any that keep to these rules, and one draw needn't show every extreme that they name: `block_table`: a group's 16 entries are distinct slots of its pool, slot s lying on pool device s // 8 of the group; in every group some pool device has all its 8 slots listed. `cached_len`: in every group some request sees all 1024 cached tokens. `request_ids`: never falling along a group's tokens; each request has 1 to 128 tokens, some request exactly 128. `routes`: each token names 8 different experts; among the 64 rows of one device no expert is named more than 32 times, a bound that some block reaches.
All inputs are finite; a program needn't handle non-finite values.
Results may differ from the reference program's by a relative error of at most 0.017.
Values may be sent and summed in bfloat16 or wider, within the bound.
No kernel may reach another device: no remote copies, remote signals or barrier semaphores. Data moves between devices by JAX's collectives and lax.ppermute only.
A program may use at most 64 MiB of HBM per device.

```python
import math
import jax
import jax.numpy as jnp
import numpy as np
from jax import lax

D = 1024
QUERY_HEADS = 16
KEY_VALUE_HEADS = 8
HEAD_SIZE = 64
EXPERTS = 32
FF = 512
TOPK = 8
TOK_DEV = 64
DEVICE_BLOCKS = 8
BLOCK_TOKENS = 64
REQS = 3
LIST = 16
GROUP_TOKENS = 256
NEW_TOKENS = 16384
CAP = 32
ESPLIT = 2
UNITS = 64
FF_UNIT = 256
N_TOK = 64
N_POOL = 4
DEVICES = 256


def fresh_pair(key):
    base = jax.random.fold_in(key, 7)
    key_query, key_entries = jax.random.split(base, 2)
    query_draw = 2.0 * jax.random.normal(key_query, (NEW_TOKENS, QUERY_HEADS * HEAD_SIZE), jnp.float32)
    paired_sample = 1.5 * jax.random.normal(key_entries, (NEW_TOKENS, 2 * KEY_VALUE_HEADS * HEAD_SIZE), jnp.float32)
    return (jnp.clip(query_draw, -2000.0, 2000.0), jnp.clip(paired_sample, -16.0, 16.0))


def draw_queries(key, part):
    return fresh_pair(key)[0].astype(jnp.bfloat16)


def draw_fresh_kv(key, part):
    return fresh_pair(key)[1].astype(jnp.bfloat16)


def draw_block_table(key, part):

    def one_row(row_key):
        key_busy, key_other, key_order = jax.random.split(row_key, 3)
        busiest = jax.random.randint(key_busy, (), 0, N_POOL)
        others = jax.random.permutation(key_other, (N_POOL - 1) * DEVICE_BLOCKS)[:LIST - DEVICE_BLOCKS].astype(jnp.int32)
        holder = others // DEVICE_BLOCKS
        holder = holder + (holder >= busiest).astype(jnp.int32)
        chosen = holder * DEVICE_BLOCKS + others % DEVICE_BLOCKS
        owned = busiest * DEVICE_BLOCKS + jnp.arange(DEVICE_BLOCKS, dtype=jnp.int32)
        listed = jnp.concatenate([owned, chosen]).astype(jnp.int32)
        return jax.random.permutation(key_order, listed)
    return jax.vmap(one_row)(jax.random.split(jax.random.fold_in(key, 3), N_TOK)).astype(jnp.int32)


def draw_cached_len(key, part):
    key_len, key_full = jax.random.split(jax.random.fold_in(key, 5))
    lengths = jax.random.randint(key_len, (N_TOK, REQS), 1, LIST * BLOCK_TOKENS + 1)
    fullest = jax.random.randint(key_full, (N_TOK, 1), 0, REQS)
    return jnp.where(jnp.arange(REQS)[None, :] == fullest, LIST * BLOCK_TOKENS, lengths).astype(jnp.int32)


def shard_levels(rng, dims, cuts, least, largest):
    def one(axis_at, shards_of):
        heights = jax.random.uniform(jax.random.fold_in(jax.random.fold_in(rng, 6), axis_at), (shards_of,), jnp.float32, least / len(cuts), largest / len(cuts))
        return jnp.repeat(jnp.exp(heights), dims[axis_at] // shards_of).reshape((-1,) + (1,) * (len(dims) - axis_at - 1))

    level = one(*cuts[0])
    for cut in cuts[1:]:
        level = level * one(*cut)
    return level


def profile(count, total, reach, lean):
    loads = [(1 << 20) // math.isqrt(grade ** lean) + 1 for grade in range(2, count + 1)]
    surplus, holding = total - reach - (count - 1), [1] * (count - 1)
    while surplus > 0:
        free = [i for i in range(count - 1) if holding[i] < reach]
        mass, budget = sum([loads[i] for i in free]), surplus
        for i in free:
            addition = min(reach - holding[i], max(1, budget * loads[i] // mass), surplus)
            holding[i] = holding[i] + addition
            surplus = surplus - addition
    return np.array([reach] + holding)


def uneven_parts(rng, number_of, total, bound, slope):
    if number_of == 2:
        one = jax.random.randint(rng, (), max(1, total - bound), min(bound, total - 1) + 1)
        return jnp.stack([one, total - one])
    sizes = jnp.asarray(profile(number_of, total, bound, slope), jnp.int32)
    couples = (number_of - 1) // 2
    giver, taker = sizes[1:1 + 2 * couples:2], sizes[2:2 + 2 * couples:2]
    margin = jnp.minimum(giver - 1, bound - taker)
    shifted = jax.random.randint(jax.random.fold_in(rng, 1), (couples,), 0, 1 << 20) % (margin + 1)
    sizes = sizes.at[1:1 + 2 * couples:2].set(giver - shifted).at[2:2 + 2 * couples:2].set(taker + shifted)
    return sizes[jax.random.permutation(jax.random.fold_in(rng, 2), number_of)]


def deal_out(own_key, own, number, rows, amount, top, most, lean):
    ranking = jax.random.permutation(own_key, amount)
    heavy_load, usual = portions_of(amount, rows * top, most, lean, True), portions_of(amount, rows * top, most, lean, False)
    places = jnp.arange(amount)

    def named(sizes, turn):
        used = int((sizes > 0).sum())
        fixed = max(1, used // 4)
        moved = fixed + (places - fixed + turn * (used - fixed)) % max(1, amount - fixed)
        return jnp.zeros((amount,), jnp.int32).at[ranking[jnp.where(places < fixed, places, moved)]].set(jnp.asarray(sizes, jnp.int32))

    sizes = jnp.where(number % 4 == 0, named(heavy_load, number // 4), named(usual, number - number // 4 - 1))
    mixed = jax.random.permutation(jax.random.fold_in(own, 3), amount)
    source_of, taker = mixed[0:amount // 2 * 2:2], mixed[1:amount // 2 * 2:2]
    room = jnp.minimum(sizes[source_of] - 1, most - sizes[taker]) // 2
    room = jnp.where((source_of == ranking[0]) | (taker == ranking[0]) | (sizes[taker] == 0), 0, jnp.maximum(room, 0))
    moved = jax.random.randint(jax.random.fold_in(own, 4), (amount // 2,), 0, 1 << 20) % (room + 1)
    sizes = sizes.at[source_of].add(-moved).at[taker].add(moved)
    members = jnp.searchsorted(jnp.cumsum(sizes), jnp.arange(rows * top), side="right").astype(jnp.int32)
    grid = members.reshape(top, rows).T
    grid = grid[jax.random.permutation(jax.random.fold_in(own, 1), rows)]
    turn = jax.random.randint(jax.random.fold_in(own, 2), (rows, 1), 0, top)
    return jnp.take_along_axis(grid, (jnp.arange(top)[None, :] + turn) % top, axis=1)


def portions_of(count, total, limit, skew, full):
    loads = [(1 << 20) // math.isqrt(grade ** skew) + 1 for grade in range(1, count + 1)]
    largest = limit if full else min(limit, max(-(-total // count), total * loads[0] // sum(loads)))
    least = 1 if total - largest >= count - 1 else 0
    counts, spare = [largest] + [least] * (count - 1), total - largest - least * (count - 1)
    while spare > 0:
        movable = [i for i in range(1, count) if counts[i] < largest] or [i for i in range(1, count) if counts[i] < limit]
        pool, remaining = sum([loads[i] for i in movable]), spare
        for i in movable:
            extra = min(limit - counts[i], max(1, remaining * loads[i] // pool), spare)
            counts[i] = counts[i] + extra
            spare = spare - extra
    return np.array(counts)


def gaussian(own_key, shape, scale, bound, pieces=(), kind=jnp.bfloat16):
    level = shard_levels(own_key, shape, pieces, -0.22, 0.18) if pieces else 1.0
    values = jax.random.normal(own_key, shape, jnp.float32) * scale * level
    return jnp.minimum(jnp.maximum(values, -bound), bound).astype(kind)


def setup_inputs(seed: int = 0) -> dict:
    arg_keys = jax.random.split(jax.random.key(seed), 14)
    stream = gaussian(arg_keys[0], (NEW_TOKENS, D), 1.0, 6.0, ((0, 256),))
    queries = draw_queries(jax.random.fold_in(arg_keys[13], 71), 0)
    fresh_kv = draw_fresh_kv(jax.random.fold_in(arg_keys[13], 71), 0)
    cache_block_pool = gaussian(arg_keys[3], (N_TOK * N_POOL * DEVICE_BLOCKS, BLOCK_TOKENS, 2 * KEY_VALUE_HEADS * HEAD_SIZE), 1.5, 9.0, ((0, 256),))
    block_table = draw_block_table(jax.random.fold_in(arg_keys[13], 71), 0)
    cached_len = draw_cached_len(jax.random.fold_in(arg_keys[13], 71), 0)
    request_ids = jax.vmap(lambda own: jnp.searchsorted(jnp.cumsum(uneven_parts(own, REQS, GROUP_TOKENS, GROUP_TOKENS // 2, 2)), jnp.arange(GROUP_TOKENS), side="right"))(jax.random.split(arg_keys[6], N_TOK)).reshape((N_TOK, GROUP_TOKENS)).astype(jnp.int32)
    output_weight = gaussian(arg_keys[7], (QUERY_HEADS * HEAD_SIZE, D), (QUERY_HEADS * HEAD_SIZE) ** -0.5, 0.1875)
    norm_gain = jnp.clip(1.0 + 0.1 * jax.random.normal(arg_keys[8], (D,), jnp.float32), 0.5, 1.5)
    expert_gate_up = gaussian(arg_keys[9], (UNITS, D, 2 * FF_UNIT), D ** -0.5, 0.1875, ((0, 64),))
    expert_down = gaussian(arg_keys[10], (UNITS, FF_UNIT, D), FF ** -0.5, 0.25, ((0, 64),))
    routes_keys = jax.random.split(jax.random.fold_in(arg_keys[11], 1), NEW_TOKENS // TOK_DEV)
    routes_turns = jax.random.permutation(jax.random.fold_in(arg_keys[11], 3), NEW_TOKENS // TOK_DEV)
    routes = jax.vmap(lambda own, number: deal_out(jax.random.fold_in(arg_keys[11], 2), own, number, TOK_DEV, EXPERTS, TOPK, CAP, 1))(routes_keys, routes_turns).reshape((NEW_TOKENS, TOPK))
    route_weight = jnp.clip(0.05 + 0.35 * jax.random.uniform(arg_keys[12], (NEW_TOKENS, TOPK), jnp.float32) ** shard_levels(arg_keys[12], (NEW_TOKENS, TOPK), ((0, 256),), -0.2, 0.2), 0.05, 0.4)
    return {"stream": stream, "queries": queries, "fresh_kv": fresh_kv, "cache_block_pool": cache_block_pool, "block_table": block_table, "cached_len": cached_len, "request_ids": request_ids, "output_weight": output_weight, "norm_gain": norm_gain, "expert_gate_up": expert_gate_up, "expert_down": expert_down, "routes": routes, "route_weight": route_weight}


score_scale = 0.015625
masked_filler = -1e+30

def reference(stream, queries, fresh_kv, cache_block_pool, block_table, cached_len, request_ids, output_weight, norm_gain, expert_gate_up, expert_down, routes, route_weight):
    heads_per_group = QUERY_HEADS // KEY_VALUE_HEADS
    key_value_width = KEY_VALUE_HEADS * HEAD_SIZE
    row_queries = queries.reshape(N_TOK, GROUP_TOKENS, QUERY_HEADS * HEAD_SIZE)
    row_fresh = fresh_kv.reshape(N_TOK, GROUP_TOKENS, 2 * key_value_width)
    row_pool = cache_block_pool.reshape(N_TOK, N_POOL * DEVICE_BLOCKS, BLOCK_TOKENS, 2 * key_value_width)

    def one_group(packed):
        group_query, group_kv, group_pool, table, lengths, segment = packed
        cached = group_pool[table].reshape(LIST * BLOCK_TOKENS, 2 * key_value_width)
        key_value_pairs = jnp.concatenate([cached, group_kv], axis=0)
        limit_len = lengths[segment]
        positions = jnp.arange(LIST * BLOCK_TOKENS, dtype=jnp.int32)
        order = jnp.arange(GROUP_TOKENS, dtype=jnp.int32)
        visible = jnp.concatenate([positions[None, :] < limit_len[:, None], (segment[None, :] == segment[:, None]) & (order[None, :] <= order[:, None])], axis=1)
        query_row_block = group_query.reshape(GROUP_TOKENS, KEY_VALUE_HEADS, heads_per_group, HEAD_SIZE).astype(jnp.float32)
        key_row_block = key_value_pairs[:, :key_value_width].reshape(-1, KEY_VALUE_HEADS, HEAD_SIZE).astype(jnp.float32)
        value_row_block = key_value_pairs[:, key_value_width:].reshape(-1, KEY_VALUE_HEADS, HEAD_SIZE).astype(jnp.float32)
        scores = jnp.einsum('qhgd,khd->qhgk', query_row_block, key_row_block, precision=lax.Precision.HIGHEST) * score_scale
        shown_keys = visible[:, None, None, :]
        scores = jnp.where(shown_keys, scores, masked_filler)
        highest = lax.optimization_barrier(jnp.max(scores, axis=-1, keepdims=True))
        weights = jnp.where(shown_keys, jnp.exp(scores - highest), 0.0)
        denominator = lax.optimization_barrier(jnp.sum(weights, axis=-1))
        rounded = lax.optimization_barrier(weights.astype(jnp.bfloat16)).astype(jnp.float32)
        summed = jnp.einsum('qhgk,khd->qhgd', rounded, value_row_block, precision=lax.Precision.HIGHEST)
        return (summed / denominator[..., None]).reshape(GROUP_TOKENS, QUERY_HEADS * HEAD_SIZE).astype(jnp.bfloat16)
    attended = lax.map(one_group, (row_queries, row_fresh, row_pool, block_table, cached_len, request_ids)).reshape(NEW_TOKENS, QUERY_HEADS * HEAD_SIZE)
    residual = stream.astype(jnp.float32) + jnp.dot(attended, output_weight, preferred_element_type=jnp.float32)
    meansq = lax.optimization_barrier(jnp.mean(residual * residual, axis=-1, keepdims=True))
    normed = (residual * lax.rsqrt(meansq + 1e-06) * norm_gain).astype(jnp.bfloat16)
    flat_routes = routes.reshape(DEVICES, TOK_DEV * TOPK)
    onehot = (flat_routes[..., None] == jnp.arange(EXPERTS, dtype=jnp.int32)).astype(jnp.int32)
    earlier = jnp.cumsum(onehot, axis=1) - onehot
    slot_of = lax.optimization_barrier(jnp.sum(earlier * onehot, axis=-1))
    device_of = jnp.arange(DEVICES, dtype=jnp.int32)[:, None]
    row_of = device_of * TOK_DEV + jnp.arange(TOK_DEV * TOPK, dtype=jnp.int32)[None, :] // TOPK
    spread = DEVICES * CAP
    place = (flat_routes * spread + device_of * CAP + slot_of).reshape(-1)
    owners = jnp.full((EXPERTS * spread,), -1, jnp.int32).at[place].set(row_of.reshape(-1))
    shares = jnp.zeros((EXPERTS * spread,), jnp.float32).at[place].set(route_weight.reshape(-1))

    def one_expert(mixed, expert):
        rows_here = lax.dynamic_slice_in_dim(owners, expert * spread, spread)
        factor = lax.dynamic_slice_in_dim(shares, expert * spread, spread)
        safe_rows = jnp.maximum(rows_here, 0)
        taken = normed[safe_rows]
        combined = jnp.zeros((spread, D), jnp.float32)
        for half in range(ESPLIT):
            unit = expert * ESPLIT + half
            gate_up = jnp.dot(taken, expert_gate_up[unit], preferred_element_type=jnp.float32)
            inner = (jax.nn.silu(gate_up[:, :FF_UNIT]) * gate_up[:, FF_UNIT:]).astype(jnp.bfloat16)
            part_out = jnp.dot(inner, expert_down[unit], preferred_element_type=jnp.float32).astype(jnp.bfloat16)
            combined = combined + lax.optimization_barrier(part_out).astype(jnp.float32)
        produced = combined.astype(jnp.bfloat16)
        mixed = mixed.at[safe_rows].add(factor[:, None] * produced.astype(jnp.float32))
        return (mixed, None)
    experts_sum, leftover = lax.scan(one_expert, jnp.zeros((NEW_TOKENS, D), jnp.float32), jnp.arange(EXPERTS, dtype=jnp.int32))
    layer_out = (residual + experts_sum).astype(jnp.bfloat16)
    return (attended, layer_out)
```

```python
import jax
import jax.numpy as jnp
from jax import lax
from jax.sharding import PartitionSpec as P

QUERY_HEADS = 16
KEY_VALUE_HEADS = 8
HEAD_SIZE = 64
EXPERTS = 32
FF = 512
TOPK = 8
CAP = 32


score_scale = 0.015625
masked_filler = -1e30


def block_group():
    for candidate in (8, 4, 2, 1):
        return candidate
    return 1


def masked_scores(query_row_block, key_value_pairs, visible):
    kv_heads = query_row_block.shape[1]
    head_dim = query_row_block.shape[3]
    key_count = key_value_pairs.shape[0]
    middle = key_value_pairs.shape[1] // 2
    key_row_block = key_value_pairs[:, :middle].reshape(key_count, kv_heads, head_dim)
    value_row_block = key_value_pairs[:, middle:].reshape(key_count, kv_heads, head_dim)
    scores = (
        jnp.einsum(
            "qhgd,khd->qhgk", query_row_block, key_row_block, preferred_element_type=jnp.float32
        )
        * score_scale
    )
    scores = jnp.where(visible[:, None, None, :], scores, masked_filler)
    return (scores, value_row_block)


def attend_update(partial_value, query_row_block, key_value_pairs, visible):
    running, denominator, summed = partial_value
    scores, value_row_block = masked_scores(query_row_block, key_value_pairs, visible)
    shown_keys = visible[:, None, None, :]
    highest = jnp.maximum(running, jnp.max(scores, axis=-1))
    rescale = jnp.exp(running - highest)
    weights = jnp.where(shown_keys, jnp.exp(scores - highest[..., None]), 0.0)
    denominator = denominator * rescale + jnp.sum(weights, axis=-1)
    product = jnp.einsum(
        "qhgk,khd->qhgd",
        weights.astype(jnp.bfloat16),
        value_row_block,
        preferred_element_type=jnp.float32,
    )
    summed = summed * rescale[..., None] + product
    return (highest, denominator, summed)


def scan_blocks(step_fn, carried, blocks, logical, limit_len):
    number = blocks.shape[0]
    block_len = blocks.shape[1]
    per_step = block_group()
    offsets = jnp.arange(block_len, dtype=jnp.int32)

    def visit(state, pieces):
        group_blocks, group_logical = pieces
        positions = (group_logical[:, None] * block_len + offsets[None, :]).reshape(-1)
        listed = jnp.repeat(group_logical >= 0, block_len)
        visible = listed[None, :] & (positions[None, :] < limit_len[:, None])
        return (step_fn(state, group_blocks.reshape(per_step * block_len, -1), visible), None)

    carried, _ = lax.scan(
        visit,
        carried,
        (
            blocks.reshape(number // per_step, per_step, block_len, -1),
            logical.reshape(number // per_step, per_step),
        ),
    )
    return carried


def pair_ffn(rows_in, gate_up_pair, down_pair):
    hidden_units = gate_up_pair.shape[2] // 2
    total = None
    for part in range(gate_up_pair.shape[0]):
        gate_up = jnp.dot(rows_in, gate_up_pair[part], preferred_element_type=jnp.float32)
        inner = (jax.nn.silu(gate_up[:, :hidden_units]) * gate_up[:, hidden_units:]).astype(
            jnp.bfloat16
        )
        produced = jnp.dot(inner, down_pair[part], preferred_element_type=jnp.float32).astype(
            jnp.bfloat16
        ).astype(jnp.float32)
        total = produced if total is None else total + produced
    return total.astype(jnp.bfloat16)


def direct_dispatch(send_rows, split, expert_gate_up, expert_down):
    width = send_rows.shape[1]
    gate_up_pair, down_pair = expert_gate_up, expert_down
    unit_rows = send_rows.reshape(EXPERTS * split, CAP // split, width)
    arrived = lax.all_to_all(unit_rows, "tok", split_axis=0, concat_axis=0, tiled=True)
    produced = pair_ffn(arrived.reshape(-1, width), gate_up_pair, down_pair)
    returned = lax.all_to_all(
        produced.reshape(EXPERTS * split, CAP // split, width),
        "tok",
        split_axis=0,
        concat_axis=0,
        tiled=True,
    )
    return returned.reshape(EXPERTS * CAP, width)


def body(
    stream,
    queries,
    fresh_kv,
    cache_block_pool,
    block_table,
    cached_len,
    request_ids,
    output_weight,
    norm_gain,
    expert_gate_up,
    expert_down,
    routes,
    route_weight,
):
    tokens_per_device = stream.shape[0]
    width = stream.shape[1]
    tok_size = lax.axis_size("tok")
    sibling = [(t, t ^ 1) for t in range(tok_size)]
    sibling_gate_up = lax.ppermute(expert_gate_up, "tok", sibling)
    sibling_down = lax.ppermute(expert_down, "tok", sibling)
    heads_per_group = QUERY_HEADS // KEY_VALUE_HEADS
    pool_size = lax.axis_size("pool")
    pool_idx = lax.axis_index("pool")
    segments = request_ids[0]
    lengths = cached_len[0]
    table = block_table[0]
    list_len = table.shape[0]
    pool_blocks = cache_block_pool.shape[0]
    slots_all = pool_size * pool_blocks
    row_start = pool_idx * tokens_per_device
    query_index = row_start + jnp.arange(tokens_per_device, dtype=jnp.int32)
    query_seg = lax.dynamic_slice_in_dim(segments, row_start, tokens_per_device)
    request_range = jnp.arange(lengths.shape[0], dtype=jnp.int32)
    row_len = jnp.sum(
        jnp.where(segments[:, None] == request_range[None, :], lengths[None, :], 0), axis=1
    )
    query_len = lax.dynamic_slice_in_dim(row_len, row_start, tokens_per_device)
    slot_block = (
        jnp.sum(
            jnp.where(
                table[None, :] == jnp.arange(slots_all, dtype=jnp.int32)[:, None],
                jnp.arange(list_len, dtype=jnp.int32)[None, :] + 1,
                0,
            ),
            axis=1,
        )
        - 1
    )
    query_row_block = queries.reshape(
        tokens_per_device, KEY_VALUE_HEADS, heads_per_group, HEAD_SIZE
    )
    start_state = (
        jnp.full((tokens_per_device, KEY_VALUE_HEADS, heads_per_group), masked_filler, jnp.float32),
        jnp.zeros((tokens_per_device, KEY_VALUE_HEADS, heads_per_group), jnp.float32),
        jnp.zeros((tokens_per_device, KEY_VALUE_HEADS, heads_per_group, HEAD_SIZE), jnp.float32),
    )
    piece = lax.all_gather(fresh_kv, "pool", axis=0, tiled=True)
    key_count = piece.shape[0]
    key_index = jnp.arange(key_count, dtype=jnp.int32)
    visible = (segments[None, :] == query_seg[:, None]) & (
        key_index[None, :] <= query_index[:, None]
    )
    fresh_state = attend_update(start_state, query_row_block, piece, visible)

    def fetch_step(partial_value, piece):

        def update_step(state, key_value_pairs, visible):
            return attend_update(state, query_row_block, key_value_pairs, visible)

        return scan_blocks(update_step, partial_value, piece, slot_block, query_len)

    gathered_pool = lax.all_gather(cache_block_pool, "pool", axis=0, tiled=True)
    _, denominator, summed = fetch_step(fresh_state, gathered_pool)
    context = summed / denominator[..., None]
    attended = context.reshape(tokens_per_device, QUERY_HEADS * HEAD_SIZE).astype(jnp.bfloat16)
    residual = stream.astype(jnp.float32) + jnp.dot(
        attended, output_weight, preferred_element_type=jnp.float32
    )
    meansq = jnp.mean(residual * residual, axis=-1, keepdims=True)
    normed = (residual * lax.rsqrt(meansq + 1e-06) * norm_gain).astype(jnp.bfloat16)
    flat_routes = routes.reshape(-1)
    onehot = (flat_routes[:, None] == jnp.arange(EXPERTS, dtype=jnp.int32)[None, :]).astype(
        jnp.int32
    )
    earlier = jnp.cumsum(onehot, axis=0) - onehot
    slot_of = jnp.sum(earlier * onehot, axis=1)
    destination = flat_routes * CAP + slot_of
    send_rows = (
        jnp.zeros((EXPERTS * CAP, width), jnp.bfloat16)
        .at[destination]
        .set(jnp.repeat(normed, TOPK, axis=0))
    )
    split = FF // (expert_gate_up.shape[2] // 2)
    expert_rows = direct_dispatch(
        send_rows,
        split,
        jnp.concatenate([expert_gate_up, sibling_gate_up], axis=0),
        jnp.concatenate([expert_down, sibling_down], axis=0),
    )
    picked = expert_rows[destination].reshape(tokens_per_device, TOPK, width)
    experts_sum = jnp.einsum("tkd,tk->td", picked.astype(jnp.float32), route_weight)
    layer_out = (residual + experts_sum).astype(jnp.bfloat16)
    return (attended, layer_out)


def solution(mesh):
    placed = (
        P(("tok", "pool"), None),
        P(("tok", "pool"), None),
        P(("tok", "pool"), None),
        P(("tok", "pool"), None, None),
        P("tok", None),
        P("tok", None),
        P("tok", None),
        P(),
        P(),
        P("tok", None, None),
        P("tok", None, None),
        P(("tok", "pool"), None),
        P(("tok", "pool"), None),
    )
    return jax.shard_map(
        body,
        mesh=mesh,
        in_specs=placed,
        out_specs=(P(("tok", "pool"), None), P(("tok", "pool"), None)),
        check_vma=False,
    )
```

```python
import jax
import jax.numpy as jnp
from jax import lax
from jax.sharding import PartitionSpec as P

QUERY_HEADS = 16
KEY_VALUE_HEADS = 8
HEAD_SIZE = 64
EXPERTS = 32
FF = 512
TOPK = 8
CAP = 32


score_scale = 0.015625
masked_filler = -1e30


def pair_ffn(rows_in, gate_up_pair, down_pair):
    hidden_units = gate_up_pair.shape[2] // 2
    total = None
    for part in range(gate_up_pair.shape[0]):
        gate_up = jnp.dot(rows_in, gate_up_pair[part], preferred_element_type=jnp.float32)
        inner = (jax.nn.silu(gate_up[:, :hidden_units]) * gate_up[:, hidden_units:]).astype(
            jnp.bfloat16
        )
        produced = jnp.dot(inner, down_pair[part], preferred_element_type=jnp.float32).astype(
            jnp.bfloat16
        ).astype(jnp.float32)
        total = produced if total is None else total + produced
    return total.astype(jnp.bfloat16)


def direct_dispatch(send_rows, split, expert_gate_up, expert_down):
    width = send_rows.shape[1]
    gate_up_pair, down_pair = expert_gate_up, expert_down
    unit_rows = send_rows.reshape(EXPERTS * split, CAP // split, width)
    arrived = lax.all_to_all(unit_rows, "tok", split_axis=0, concat_axis=0, tiled=True)
    produced = pair_ffn(arrived.reshape(-1, width), gate_up_pair, down_pair)
    returned = lax.all_to_all(
        produced.reshape(EXPERTS * split, CAP // split, width),
        "tok",
        split_axis=0,
        concat_axis=0,
        tiled=True,
    )
    return returned.reshape(EXPERTS * CAP, width)


def body(
    stream,
    queries,
    fresh_kv,
    cache_block_pool,
    block_table,
    cached_len,
    request_ids,
    output_weight,
    norm_gain,
    expert_gate_up,
    expert_down,
    routes,
    route_weight,
):
    tokens_per_device = stream.shape[0]
    width = stream.shape[1]
    tok_size = lax.axis_size("tok")
    sibling = [(t, t ^ 1) for t in range(tok_size)]
    sibling_gate_up = lax.ppermute(expert_gate_up, "tok", sibling)
    sibling_down = lax.ppermute(expert_down, "tok", sibling)
    heads_per_group = QUERY_HEADS // KEY_VALUE_HEADS
    kv_width = KEY_VALUE_HEADS * HEAD_SIZE
    pool_size = lax.axis_size("pool")
    pool_idx = lax.axis_index("pool")
    segments = request_ids[0]
    lengths = cached_len[0]
    table = block_table[0]
    list_len = table.shape[0]
    pool_blocks = cache_block_pool.shape[0]
    block_len = cache_block_pool.shape[1]
    group_tokens = segments.shape[0]
    request_range = jnp.arange(lengths.shape[0], dtype=jnp.int32)
    row_len = jnp.sum(
        jnp.where(segments[:, None] == request_range[None, :], lengths[None, :], 0), axis=1
    )
    local_slots = pool_idx * pool_blocks + jnp.arange(pool_blocks, dtype=jnp.int32)
    slot_block = (
        jnp.sum(
            jnp.where(
                table[None, :] == local_slots[:, None],
                jnp.arange(list_len, dtype=jnp.int32)[None, :] + 1,
                0,
            ),
            axis=1,
        )
        - 1
    )
    offsets = jnp.arange(block_len, dtype=jnp.int32)
    cache_pos = (slot_block[:, None] * block_len + offsets[None, :]).reshape(-1)
    cache_listed = jnp.repeat(slot_block >= 0, block_len)
    cache_visible = cache_listed[None, :] & (cache_pos[None, :] < row_len[:, None])
    query_order = jnp.arange(group_tokens, dtype=jnp.int32)
    fresh_order = pool_idx * tokens_per_device + jnp.arange(tokens_per_device, dtype=jnp.int32)
    fresh_seg = lax.dynamic_slice_in_dim(segments, pool_idx * tokens_per_device, tokens_per_device)
    fresh_visible = (fresh_seg[None, :] == segments[:, None]) & (
        fresh_order[None, :] <= query_order[:, None]
    )
    visible = jnp.concatenate([cache_visible, fresh_visible], axis=1)
    group_queries = lax.all_gather(queries, "pool", axis=0, tiled=True)
    key_value_pairs = jnp.concatenate(
        [cache_block_pool.reshape(pool_blocks * block_len, 2 * kv_width), fresh_kv], axis=0
    )
    key_count = key_value_pairs.shape[0]
    query_row_block = group_queries.reshape(
        group_tokens, KEY_VALUE_HEADS, heads_per_group, HEAD_SIZE
    )
    key_row_block = key_value_pairs[:, :kv_width].reshape(key_count, KEY_VALUE_HEADS, HEAD_SIZE)
    value_row_block = key_value_pairs[:, kv_width:].reshape(key_count, KEY_VALUE_HEADS, HEAD_SIZE)
    scores = (
        jnp.einsum(
            "qhgd,khd->qhgk",
            query_row_block,
            key_row_block,
            preferred_element_type=jnp.float32,
        )
        * score_scale
    )
    shown_keys = visible[:, None, None, :]
    scores = jnp.where(shown_keys, scores, masked_filler)
    highest = jnp.max(scores, axis=-1)
    weights = jnp.where(shown_keys, jnp.exp(scores - highest[..., None]), 0.0)
    denominator = jnp.sum(weights, axis=-1)
    summed = jnp.einsum(
        "qhgk,khd->qhgd",
        weights.astype(jnp.bfloat16),
        value_row_block,
        preferred_element_type=jnp.float32,
    )
    partial = jnp.concatenate(
        [summed, highest[..., None], denominator[..., None]], axis=-1
    ).reshape(pool_size, tokens_per_device, -1)
    gathered = lax.all_to_all(partial, "pool", split_axis=0, concat_axis=0, tiled=True).reshape(
        pool_size, tokens_per_device, KEY_VALUE_HEADS, heads_per_group, HEAD_SIZE + 2
    )
    part_max = gathered[..., HEAD_SIZE]
    running = jnp.max(part_max, axis=0)
    rescale = jnp.exp(part_max - running[None])
    denominator = jnp.sum(gathered[..., HEAD_SIZE + 1] * rescale, axis=0)
    summed = jnp.sum(gathered[..., :HEAD_SIZE] * rescale[..., None], axis=0)
    context = summed / denominator[..., None]
    attended = context.reshape(tokens_per_device, QUERY_HEADS * HEAD_SIZE).astype(jnp.bfloat16)
    residual = stream.astype(jnp.float32) + jnp.dot(
        attended, output_weight, preferred_element_type=jnp.float32
    )
    meansq = jnp.mean(residual * residual, axis=-1, keepdims=True)
    normed = (residual * lax.rsqrt(meansq + 1e-06) * norm_gain).astype(jnp.bfloat16)
    flat_routes = routes.reshape(-1)
    onehot = (flat_routes[:, None] == jnp.arange(EXPERTS, dtype=jnp.int32)[None, :]).astype(
        jnp.int32
    )
    earlier = jnp.cumsum(onehot, axis=0) - onehot
    slot_of = jnp.sum(earlier * onehot, axis=1)
    destination = flat_routes * CAP + slot_of
    send_rows = (
        jnp.zeros((EXPERTS * CAP, width), jnp.bfloat16)
        .at[destination]
        .set(jnp.repeat(normed, TOPK, axis=0))
    )
    split = FF // (expert_gate_up.shape[2] // 2)
    expert_rows = direct_dispatch(
        send_rows,
        split,
        jnp.concatenate([expert_gate_up, sibling_gate_up], axis=0),
        jnp.concatenate([expert_down, sibling_down], axis=0),
    )
    picked = expert_rows[destination].reshape(tokens_per_device, TOPK, width)
    experts_sum = jnp.einsum("tkd,tk->td", picked.astype(jnp.float32), route_weight)
    layer_out = (residual + experts_sum).astype(jnp.bfloat16)
    return (attended, layer_out)


def solution(mesh):
    placed = (
        P(("tok", "pool"), None),
        P(("tok", "pool"), None),
        P(("tok", "pool"), None),
        P(("tok", "pool"), None, None),
        P("tok", None),
        P("tok", None),
        P("tok", None),
        P(),
        P(),
        P("tok", None, None),
        P("tok", None, None),
        P(("tok", "pool"), None),
        P(("tok", "pool"), None),
    )
    return jax.shard_map(
        body,
        mesh=mesh,
        in_specs=placed,
        out_specs=(P(("tok", "pool"), None), P(("tok", "pool"), None)),
        check_vma=False,
    )
```

```python
import jax
import jax.numpy as jnp
from jax import lax
from jax.sharding import PartitionSpec as P

QUERY_HEADS = 16
KEY_VALUE_HEADS = 8
HEAD_SIZE = 64
EXPERTS = 32
FF = 512
TOPK = 8
CAP = 32


score_scale = 0.015625
masked_filler = -1e30


def pair_ffn(rows_in, gate_up_pair, down_pair):
    hidden_units = gate_up_pair.shape[2] // 2
    total = None
    for part in range(gate_up_pair.shape[0]):
        gate_up = jnp.dot(rows_in, gate_up_pair[part], preferred_element_type=jnp.float32)
        inner = (jax.nn.silu(gate_up[:, :hidden_units]) * gate_up[:, hidden_units:]).astype(
            jnp.bfloat16
        )
        produced = jnp.dot(inner, down_pair[part], preferred_element_type=jnp.float32).astype(
            jnp.bfloat16
        ).astype(jnp.float32)
        total = produced if total is None else total + produced
    return total.astype(jnp.bfloat16)


def direct_dispatch(send_rows, split, expert_gate_up, expert_down):
    width = send_rows.shape[1]
    gate_up_pair, down_pair = expert_gate_up, expert_down
    unit_rows = send_rows.reshape(EXPERTS * split, CAP // split, width)
    arrived = lax.all_to_all(unit_rows, "tok", split_axis=0, concat_axis=0, tiled=True)
    produced = pair_ffn(arrived.reshape(-1, width), gate_up_pair, down_pair)
    returned = lax.all_to_all(
        produced.reshape(EXPERTS * split, CAP // split, width),
        "tok",
        split_axis=0,
        concat_axis=0,
        tiled=True,
    )
    return returned.reshape(EXPERTS * CAP, width)


def body(
    stream,
    queries,
    fresh_kv,
    cache_block_pool,
    block_table,
    cached_len,
    request_ids,
    output_weight,
    norm_gain,
    expert_gate_up,
    expert_down,
    routes,
    route_weight,
):
    tokens_per_device = stream.shape[0]
    width = stream.shape[1]
    tok_size = lax.axis_size("tok")
    sibling = [(t, t ^ 1) for t in range(tok_size)]
    sibling_gate_up = lax.ppermute(expert_gate_up, "tok", sibling)
    sibling_down = lax.ppermute(expert_down, "tok", sibling)
    heads_per_group = QUERY_HEADS // KEY_VALUE_HEADS
    kv_width = KEY_VALUE_HEADS * HEAD_SIZE
    pool_size = lax.axis_size("pool")
    pool_idx = lax.axis_index("pool")
    segments = request_ids[0]
    lengths = cached_len[0]
    table = block_table[0]
    list_len = table.shape[0]
    pool_blocks = cache_block_pool.shape[0]
    block_len = cache_block_pool.shape[1]
    group_tokens = segments.shape[0]
    request_range = jnp.arange(lengths.shape[0], dtype=jnp.int32)
    row_len = jnp.sum(
        jnp.where(segments[:, None] == request_range[None, :], lengths[None, :], 0), axis=1
    )
    local_slots = pool_idx * pool_blocks + jnp.arange(pool_blocks, dtype=jnp.int32)
    slot_block = (
        jnp.sum(
            jnp.where(
                table[None, :] == local_slots[:, None],
                jnp.arange(list_len, dtype=jnp.int32)[None, :] + 1,
                0,
            ),
            axis=1,
        )
        - 1
    )
    offsets = jnp.arange(block_len, dtype=jnp.int32)
    cache_pos = (slot_block[:, None] * block_len + offsets[None, :]).reshape(-1)
    cache_listed = jnp.repeat(slot_block >= 0, block_len)
    shifts = range(pool_size)
    block_source = [(pool_idx - shift) % pool_size for shift in shifts]
    query_order = (
        jnp.stack(block_source)[:, None] * tokens_per_device
        + jnp.arange(tokens_per_device, dtype=jnp.int32)[None, :]
    ).reshape(-1)
    query_seg = segments[query_order]
    query_len = row_len[query_order]
    cache_visible = cache_listed[None, :] & (cache_pos[None, :] < query_len[:, None])
    fresh_order = pool_idx * tokens_per_device + jnp.arange(tokens_per_device, dtype=jnp.int32)
    fresh_seg = lax.dynamic_slice_in_dim(segments, pool_idx * tokens_per_device, tokens_per_device)
    fresh_visible = (fresh_seg[None, :] == query_seg[:, None]) & (
        fresh_order[None, :] <= query_order[:, None]
    )
    visible = jnp.concatenate([cache_visible, fresh_visible], axis=1)
    query_blocks = [queries] + [
        lax.ppermute(
            queries, "pool", [(i, (i + shift) % pool_size) for i in range(pool_size)]
        )
        for shift in shifts[1:]
    ]
    group_queries = jnp.concatenate(query_blocks, axis=0)
    key_value_pairs = jnp.concatenate(
        [cache_block_pool.reshape(pool_blocks * block_len, 2 * kv_width), fresh_kv], axis=0
    )
    key_count = key_value_pairs.shape[0]
    query_row_block = group_queries.reshape(
        group_tokens, KEY_VALUE_HEADS, heads_per_group, HEAD_SIZE
    )
    key_row_block = key_value_pairs[:, :kv_width].reshape(key_count, KEY_VALUE_HEADS, HEAD_SIZE)
    value_row_block = key_value_pairs[:, kv_width:].reshape(key_count, KEY_VALUE_HEADS, HEAD_SIZE)
    scores = (
        jnp.einsum(
            "qhgd,khd->qhgk",
            query_row_block,
            key_row_block,
            preferred_element_type=jnp.float32,
        )
        * score_scale
    )
    shown_keys = visible[:, None, None, :]
    scores = jnp.where(shown_keys, scores, masked_filler)
    highest = jnp.max(scores, axis=-1)
    weights = jnp.where(shown_keys, jnp.exp(scores - highest[..., None]), 0.0)
    denominator = jnp.sum(weights, axis=-1)
    summed = jnp.einsum(
        "qhgk,khd->qhgd",
        weights.astype(jnp.bfloat16),
        value_row_block,
        preferred_element_type=jnp.float32,
    )
    stat_pad = 128 - 2 * QUERY_HEADS
    partial = jnp.concatenate(
        [
            summed.reshape(group_tokens, QUERY_HEADS * HEAD_SIZE),
            highest.reshape(group_tokens, QUERY_HEADS),
            denominator.reshape(group_tokens, QUERY_HEADS),
            jnp.zeros((group_tokens, stat_pad), jnp.float32),
        ],
        axis=1,
    ).reshape(pool_size, tokens_per_device, -1)
    partials = [partial[0]] + [
        lax.ppermute(
            partial[shift], "pool", [(i, (i - shift) % pool_size) for i in range(pool_size)]
        )
        for shift in shifts[1:]
    ]
    gathered = jnp.stack(partials)
    acc_width = QUERY_HEADS * HEAD_SIZE
    part_max = gathered[:, :, acc_width : acc_width + QUERY_HEADS]
    part_sum = gathered[:, :, acc_width + QUERY_HEADS : acc_width + 2 * QUERY_HEADS]
    running = jnp.max(part_max, axis=0)
    rescale = jnp.exp(part_max - running[None])
    denominator = jnp.sum(part_sum * rescale, axis=0)
    summed = jnp.sum(
        gathered[:, :, :acc_width] * jnp.repeat(rescale, HEAD_SIZE, axis=2), axis=0
    )
    denominator = jnp.repeat(denominator, HEAD_SIZE, axis=1)
    context = summed / denominator
    attended = context.reshape(tokens_per_device, QUERY_HEADS * HEAD_SIZE).astype(jnp.bfloat16)
    residual = stream.astype(jnp.float32) + jnp.dot(
        attended, output_weight, preferred_element_type=jnp.float32
    )
    meansq = jnp.mean(residual * residual, axis=-1, keepdims=True)
    normed = (residual * lax.rsqrt(meansq + 1e-06) * norm_gain).astype(jnp.bfloat16)
    flat_routes = routes.reshape(-1)
    onehot = (flat_routes[:, None] == jnp.arange(EXPERTS, dtype=jnp.int32)[None, :]).astype(
        jnp.int32
    )
    earlier = jnp.cumsum(onehot, axis=0) - onehot
    slot_of = jnp.sum(earlier * onehot, axis=1)
    destination = flat_routes * CAP + slot_of
    send_rows = (
        jnp.zeros((EXPERTS * CAP, width), jnp.bfloat16)
        .at[destination]
        .set(jnp.repeat(normed, TOPK, axis=0))
    )
    split = FF // (expert_gate_up.shape[2] // 2)
    expert_rows = direct_dispatch(
        send_rows,
        split,
        jnp.concatenate([expert_gate_up, sibling_gate_up], axis=0),
        jnp.concatenate([expert_down, sibling_down], axis=0),
    )
    picked = expert_rows[destination].reshape(tokens_per_device, TOPK, width)
    experts_sum = jnp.einsum("tkd,tk->td", picked.astype(jnp.float32), route_weight)
    layer_out = (residual + experts_sum).astype(jnp.bfloat16)
    return (attended, layer_out)


def solution(mesh):
    placed = (
        P(("tok", "pool"), None),
        P(("tok", "pool"), None),
        P(("tok", "pool"), None),
        P(("tok", "pool"), None, None),
        P("tok", None),
        P("tok", None),
        P("tok", None),
        P(),
        P(),
        P("tok", None, None),
        P("tok", None, None),
        P(("tok", "pool"), None),
        P(("tok", "pool"), None),
    )
    return jax.shard_map(
        body,
        mesh=mesh,
        in_specs=placed,
        out_specs=(P(("tok", "pool"), None), P(("tok", "pool"), None)),
        check_vma=False,
    )
```

```python
import jax
import jax.numpy as jnp
from jax import lax
from jax.sharding import PartitionSpec as P

QUERY_HEADS = 16
KEY_VALUE_HEADS = 8
HEAD_SIZE = 64
EXPERTS = 32
FF = 512
TOPK = 8
CAP = 32


score_scale = 0.015625
masked_filler = -1e30


def pair_ffn(rows_in, gate_up_pair, down_pair):
    hidden_units = gate_up_pair.shape[2] // 2
    total = None
    for part in range(gate_up_pair.shape[0]):
        gate_up = jnp.dot(rows_in, gate_up_pair[part], preferred_element_type=jnp.float32)
        inner = (jax.nn.silu(gate_up[:, :hidden_units]) * gate_up[:, hidden_units:]).astype(
            jnp.bfloat16
        )
        produced = jnp.dot(inner, down_pair[part], preferred_element_type=jnp.float32).astype(
            jnp.bfloat16
        ).astype(jnp.float32)
        total = produced if total is None else total + produced
    return total.astype(jnp.bfloat16)


def direct_dispatch(send_rows, split, expert_gate_up, expert_down):
    width = send_rows.shape[1]
    gate_up_pair, down_pair = expert_gate_up, expert_down
    unit_rows = send_rows.reshape(EXPERTS * split, CAP // split, width)
    arrived = lax.all_to_all(unit_rows, "tok", split_axis=0, concat_axis=0, tiled=True)
    produced = pair_ffn(arrived.reshape(-1, width), gate_up_pair, down_pair)
    returned = lax.all_to_all(
        produced.reshape(EXPERTS * split, CAP // split, width),
        "tok",
        split_axis=0,
        concat_axis=0,
        tiled=True,
    )
    return returned.reshape(EXPERTS * CAP, width)


def body(
    stream,
    queries,
    fresh_kv,
    cache_block_pool,
    block_table,
    cached_len,
    request_ids,
    output_weight,
    norm_gain,
    expert_gate_up,
    expert_down,
    routes,
    route_weight,
):
    tokens_per_device = stream.shape[0]
    tok_size = lax.axis_size("tok")
    sibling = [(t, t ^ 1) for t in range(tok_size)]
    sibling_gate_up = lax.ppermute(expert_gate_up, "tok", sibling)
    sibling_down = lax.ppermute(expert_down, "tok", sibling)
    heads_per_group = QUERY_HEADS // KEY_VALUE_HEADS
    kv_width = KEY_VALUE_HEADS * HEAD_SIZE
    pool_size = lax.axis_size("pool")
    pool_idx = lax.axis_index("pool")
    segments = request_ids[0]
    lengths = cached_len[0]
    table = block_table[0]
    list_len = table.shape[0]
    pool_blocks = cache_block_pool.shape[0]
    block_len = cache_block_pool.shape[1]
    request_range = jnp.arange(lengths.shape[0], dtype=jnp.int32)
    row_len = jnp.sum(
        jnp.where(segments[:, None] == request_range[None, :], lengths[None, :], 0), axis=1
    )
    local_slots = pool_idx * pool_blocks + jnp.arange(pool_blocks, dtype=jnp.int32)
    slot_block = (
        jnp.sum(
            jnp.where(
                table[None, :] == local_slots[:, None],
                jnp.arange(list_len, dtype=jnp.int32)[None, :] + 1,
                0,
            ),
            axis=1,
        )
        - 1
    )
    offsets = jnp.arange(block_len, dtype=jnp.int32)
    cache_pos = (slot_block[:, None] * block_len + offsets[None, :]).reshape(-1)
    cache_listed = jnp.repeat(slot_block >= 0, block_len)
    shifts = range(pool_size)
    fresh_order = pool_idx * tokens_per_device + jnp.arange(tokens_per_device, dtype=jnp.int32)
    fresh_seg = lax.dynamic_slice_in_dim(segments, pool_idx * tokens_per_device, tokens_per_device)
    key_value_pairs = jnp.concatenate(
        [cache_block_pool.reshape(pool_blocks * block_len, 2 * kv_width), fresh_kv], axis=0
    )
    key_count = key_value_pairs.shape[0]
    key_row_block = key_value_pairs[:, :kv_width].reshape(key_count, KEY_VALUE_HEADS, HEAD_SIZE)
    value_row_block = key_value_pairs[:, kv_width:].reshape(key_count, KEY_VALUE_HEADS, HEAD_SIZE)
    stat_pad = 128 - 2 * QUERY_HEADS

    def attend_block(query_block, source):
        first = source * tokens_per_device
        query_order = first + jnp.arange(tokens_per_device, dtype=jnp.int32)
        query_seg = lax.dynamic_slice_in_dim(segments, first, tokens_per_device)
        query_len = lax.dynamic_slice_in_dim(row_len, first, tokens_per_device)
        cache_visible = cache_listed[None, :] & (cache_pos[None, :] < query_len[:, None])
        fresh_visible = (fresh_seg[None, :] == query_seg[:, None]) & (
            fresh_order[None, :] <= query_order[:, None]
        )
        visible = jnp.concatenate([cache_visible, fresh_visible], axis=1)
        query_row_block = query_block.reshape(
            tokens_per_device, KEY_VALUE_HEADS, heads_per_group, HEAD_SIZE
        )
        scores = (
            jnp.einsum(
                "qhgd,khd->qhgk",
                query_row_block,
                key_row_block,
                preferred_element_type=jnp.float32,
            )
            * score_scale
        )
        shown_keys = visible[:, None, None, :]
        scores = jnp.where(shown_keys, scores, masked_filler)
        highest = jnp.max(scores, axis=-1)
        weights = jnp.where(shown_keys, jnp.exp(scores - highest[..., None]), 0.0)
        denominator = jnp.sum(weights, axis=-1)
        summed = jnp.einsum(
            "qhgk,khd->qhgd",
            weights.astype(jnp.bfloat16),
            value_row_block,
            preferred_element_type=jnp.float32,
        )
        return jnp.concatenate(
            [
                summed.reshape(tokens_per_device, QUERY_HEADS * HEAD_SIZE),
                highest.reshape(tokens_per_device, QUERY_HEADS),
                denominator.reshape(tokens_per_device, QUERY_HEADS),
                jnp.zeros((tokens_per_device, stat_pad), jnp.float32),
            ],
            axis=1,
        )

    query_blocks = [queries] + [
        lax.ppermute(
            queries, "pool", [(i, (i + shift) % pool_size) for i in range(pool_size)]
        )
        for shift in shifts[1:]
    ]
    partials = [None] * pool_size
    for shift in list(shifts[1:]) + [0]:
        partial = attend_block(query_blocks[shift], (pool_idx - shift) % pool_size)
        if shift:
            partial = lax.ppermute(
                partial, "pool", [(i, (i - shift) % pool_size) for i in range(pool_size)]
            )
        partials[shift] = partial
    gathered = jnp.stack(partials)
    acc_width = QUERY_HEADS * HEAD_SIZE
    part_max = gathered[:, :, acc_width : acc_width + QUERY_HEADS]
    part_sum = gathered[:, :, acc_width + QUERY_HEADS : acc_width + 2 * QUERY_HEADS]
    running = jnp.max(part_max, axis=0)
    rescale = jnp.exp(part_max - running[None])
    denominator = jnp.sum(part_sum * rescale, axis=0)
    summed = jnp.sum(
        gathered[:, :, :acc_width] * jnp.repeat(rescale, HEAD_SIZE, axis=2), axis=0
    )
    denominator = jnp.repeat(denominator, HEAD_SIZE, axis=1)
    context = summed / denominator
    attended = context.reshape(tokens_per_device, QUERY_HEADS * HEAD_SIZE).astype(jnp.bfloat16)
    residual = stream.astype(jnp.float32) + jnp.dot(
        attended, output_weight, preferred_element_type=jnp.float32
    )
    meansq = jnp.mean(residual * residual, axis=-1, keepdims=True)
    normed = (residual * lax.rsqrt(meansq + 1e-06) * norm_gain).astype(jnp.bfloat16)
    flat_routes = routes.reshape(-1)
    onehot = (flat_routes[:, None] == jnp.arange(EXPERTS, dtype=jnp.int32)[None, :]).astype(
        jnp.int32
    )
    earlier = jnp.cumsum(onehot, axis=0) - onehot
    slot_of = jnp.sum(earlier * onehot, axis=1)
    destination = flat_routes * CAP + slot_of
    slot_range = jnp.arange(EXPERTS * CAP, dtype=jnp.int32)
    placed = destination.reshape(tokens_per_device, TOPK)[None, :, :] == slot_range[:, None, None]
    send_rows = jnp.dot(
        jnp.any(placed, axis=2).astype(jnp.bfloat16), normed, preferred_element_type=jnp.float32
    ).astype(jnp.bfloat16)
    split = FF // (expert_gate_up.shape[2] // 2)
    expert_rows = direct_dispatch(
        send_rows,
        split,
        jnp.concatenate([expert_gate_up, sibling_gate_up], axis=0),
        jnp.concatenate([expert_down, sibling_down], axis=0),
    )
    mixing = jnp.sum(jnp.where(placed, route_weight[None, :, :], 0.0), axis=2).T
    experts_sum = jnp.dot(
        mixing,
        expert_rows.astype(jnp.float32),
        precision=lax.Precision.HIGHEST,
        preferred_element_type=jnp.float32,
    )
    layer_out = (residual + experts_sum).astype(jnp.bfloat16)
    return (attended, layer_out)


def solution(mesh):
    placed = (
        P(("tok", "pool"), None),
        P(("tok", "pool"), None),
        P(("tok", "pool"), None),
        P(("tok", "pool"), None, None),
        P("tok", None),
        P("tok", None),
        P("tok", None),
        P(),
        P(),
        P("tok", None, None),
        P("tok", None, None),
        P(("tok", "pool"), None),
        P(("tok", "pool"), None),
    )
    return jax.shard_map(
        body,
        mesh=mesh,
        in_specs=placed,
        out_specs=(P(("tok", "pool"), None), P(("tok", "pool"), None)),
        check_vma=False,
    )
```

```python
import jax
import jax.numpy as jnp
from jax import lax
from jax.experimental import pallas as pl
from jax.experimental.pallas import tpu as pltpu
from jax.sharding import PartitionSpec as P

QUERY_HEADS = 16
KEY_VALUE_HEADS = 8
HEAD_SIZE = 64
EXPERTS = 32
FF = 512
TOPK = 8
CAP = 32


score_scale = 0.015625
masked_filler = -1e30


def _attend_kernel(q_ref, kv_ref, mask_ref, out_ref):
    rows = q_ref.shape[0]
    visible = mask_ref[...] > 0.5
    lane = lax.broadcasted_iota(jnp.int32, (rows, 128), 1)
    low_half = lane < HEAD_SIZE
    stats = jnp.zeros((rows, 128), jnp.float32)
    for h in range(KEY_VALUE_HEADS):
        q_tile = q_ref[:, h * 128:(h + 1) * 128].astype(jnp.float32)
        k_tile = kv_ref[:, (h // 2) * 128:(h // 2 + 1) * 128]
        v_tile = kv_ref[:, KEY_VALUE_HEADS * HEAD_SIZE + (h // 2) * 128:KEY_VALUE_HEADS * HEAD_SIZE + (h // 2 + 1) * 128]
        out_tile = jnp.zeros((rows, 128), jnp.float32)
        for g in range(2):
            j = 2 * h + g
            q_half = jnp.where(low_half if g == 0 else ~low_half, q_tile, 0.0)
            if g != h % 2:
                q_half = pltpu.roll(q_half, HEAD_SIZE, 1)
            if h % 2 == 0:
                q_half = jnp.where(low_half, q_half, 0.0)
            else:
                q_half = jnp.where(low_half, 0.0, q_half)
            scores = lax.dot_general(
                q_half.astype(jnp.bfloat16), k_tile, (((1,), (1,)), ((), ())),
                preferred_element_type=jnp.float32) * score_scale
            scores = jnp.where(visible, scores, masked_filler)
            highest = jnp.max(scores, axis=1, keepdims=True)
            weights = jnp.where(visible, jnp.exp(scores - highest), 0.0)
            total = jnp.sum(weights, axis=1, keepdims=True)
            acc = jnp.dot(weights.astype(jnp.bfloat16), v_tile, preferred_element_type=jnp.float32)
            if g != h % 2:
                acc = pltpu.roll(acc, HEAD_SIZE, 1)
            out_tile = jnp.where(low_half if g == 0 else ~low_half, acc, out_tile)
            stats = jnp.where(lane == j, highest, stats)
            stats = jnp.where(lane == QUERY_HEADS + j, total, stats)
        out_ref[:, h * 128:(h + 1) * 128] = out_tile
    out_ref[:, QUERY_HEADS * HEAD_SIZE:QUERY_HEADS * HEAD_SIZE + 128] = stats


def attend_partial(q_block, kv, mask):
    rows = q_block.shape[0]
    return pl.pallas_call(
        _attend_kernel,
        out_shape=jax.ShapeDtypeStruct((rows, QUERY_HEADS * HEAD_SIZE + 128), jnp.float32),
    )(q_block, kv, mask)


def pair_ffn(rows_in, gate_up_pair, down_pair):
    hidden_units = gate_up_pair.shape[2] // 2
    total = None
    for part in range(gate_up_pair.shape[0]):
        gate_up = jnp.dot(rows_in, gate_up_pair[part], preferred_element_type=jnp.float32)
        inner = (jax.nn.silu(gate_up[:, :hidden_units]) * gate_up[:, hidden_units:]).astype(
            jnp.bfloat16
        )
        produced = jnp.dot(inner, down_pair[part], preferred_element_type=jnp.float32).astype(
            jnp.bfloat16
        ).astype(jnp.float32)
        total = produced if total is None else total + produced
    return total.astype(jnp.bfloat16)


def direct_dispatch(send_rows, split, expert_gate_up, expert_down):
    width = send_rows.shape[1]
    gate_up_pair, down_pair = expert_gate_up, expert_down
    unit_rows = send_rows.reshape(EXPERTS * split, CAP // split, width)
    arrived = lax.all_to_all(unit_rows, "tok", split_axis=0, concat_axis=0, tiled=True)
    produced = pair_ffn(arrived.reshape(-1, width), gate_up_pair, down_pair)
    returned = lax.all_to_all(
        produced.reshape(EXPERTS * split, CAP // split, width),
        "tok",
        split_axis=0,
        concat_axis=0,
        tiled=True,
    )
    return returned.reshape(EXPERTS * CAP, width)


def body(
    stream,
    queries,
    fresh_kv,
    cache_block_pool,
    block_table,
    cached_len,
    request_ids,
    output_weight,
    norm_gain,
    expert_gate_up,
    expert_down,
    routes,
    route_weight,
):
    tokens_per_device = stream.shape[0]
    tok_size = lax.axis_size("tok")
    sibling = [(t, t ^ 1) for t in range(tok_size)]
    sibling_gate_up = lax.ppermute(expert_gate_up, "tok", sibling)
    sibling_down = lax.ppermute(expert_down, "tok", sibling)
    kv_width = KEY_VALUE_HEADS * HEAD_SIZE
    pool_size = lax.axis_size("pool")
    pool_idx = lax.axis_index("pool")
    segments = request_ids[0]
    lengths = cached_len[0]
    table = block_table[0]
    list_len = table.shape[0]
    pool_blocks = cache_block_pool.shape[0]
    block_len = cache_block_pool.shape[1]
    request_range = jnp.arange(lengths.shape[0], dtype=jnp.int32)
    row_len = jnp.sum(
        jnp.where(segments[:, None] == request_range[None, :], lengths[None, :], 0), axis=1
    )
    local_slots = pool_idx * pool_blocks + jnp.arange(pool_blocks, dtype=jnp.int32)
    slot_block = (
        jnp.sum(
            jnp.where(
                table[None, :] == local_slots[:, None],
                jnp.arange(list_len, dtype=jnp.int32)[None, :] + 1,
                0,
            ),
            axis=1,
        )
        - 1
    )
    offsets = jnp.arange(block_len, dtype=jnp.int32)
    cache_pos = (slot_block[:, None] * block_len + offsets[None, :]).reshape(-1)
    cache_listed = jnp.repeat(slot_block >= 0, block_len)
    shifts = range(pool_size)
    fresh_order = pool_idx * tokens_per_device + jnp.arange(tokens_per_device, dtype=jnp.int32)
    fresh_seg = lax.dynamic_slice_in_dim(segments, pool_idx * tokens_per_device, tokens_per_device)
    key_value_pairs = jnp.concatenate(
        [cache_block_pool.reshape(pool_blocks * block_len, 2 * kv_width), fresh_kv], axis=0
    )

    def attend_block(query_block, source):
        first = source * tokens_per_device
        query_order = first + jnp.arange(tokens_per_device, dtype=jnp.int32)
        query_seg = lax.dynamic_slice_in_dim(segments, first, tokens_per_device)
        query_len = lax.dynamic_slice_in_dim(row_len, first, tokens_per_device)
        cache_visible = cache_listed[None, :] & (cache_pos[None, :] < query_len[:, None])
        fresh_visible = (fresh_seg[None, :] == query_seg[:, None]) & (
            fresh_order[None, :] <= query_order[:, None]
        )
        visible = jnp.concatenate([cache_visible, fresh_visible], axis=1)
        return attend_partial(query_block, key_value_pairs, visible.astype(jnp.float32))

    query_blocks = [queries] + [
        lax.ppermute(
            queries, "pool", [(i, (i + shift) % pool_size) for i in range(pool_size)]
        )
        for shift in shifts[1:]
    ]
    partials = [None] * pool_size
    for shift in list(shifts[1:]) + [0]:
        partial = attend_block(query_blocks[shift], (pool_idx - shift) % pool_size)
        if shift:
            partial = lax.ppermute(
                partial, "pool", [(i, (i - shift) % pool_size) for i in range(pool_size)]
            )
        partials[shift] = partial
    gathered = jnp.stack(partials)
    acc_width = QUERY_HEADS * HEAD_SIZE
    part_max = gathered[:, :, acc_width : acc_width + QUERY_HEADS]
    part_sum = gathered[:, :, acc_width + QUERY_HEADS : acc_width + 2 * QUERY_HEADS]
    running = jnp.max(part_max, axis=0)
    rescale = jnp.exp(part_max - running[None])
    denominator = jnp.sum(part_sum * rescale, axis=0)
    summed = jnp.sum(
        gathered[:, :, :acc_width] * jnp.repeat(rescale, HEAD_SIZE, axis=2), axis=0
    )
    denominator = jnp.repeat(denominator, HEAD_SIZE, axis=1)
    context = summed / denominator
    attended = context.reshape(tokens_per_device, QUERY_HEADS * HEAD_SIZE).astype(jnp.bfloat16)
    residual = stream.astype(jnp.float32) + jnp.dot(
        attended, output_weight, preferred_element_type=jnp.float32
    )
    meansq = jnp.mean(residual * residual, axis=-1, keepdims=True)
    normed = (residual * lax.rsqrt(meansq + 1e-06) * norm_gain).astype(jnp.bfloat16)
    flat_routes = routes.reshape(-1)
    onehot = (flat_routes[:, None] == jnp.arange(EXPERTS, dtype=jnp.int32)[None, :]).astype(
        jnp.int32
    )
    earlier = jnp.cumsum(onehot, axis=0) - onehot
    slot_of = jnp.sum(earlier * onehot, axis=1)
    destination = flat_routes * CAP + slot_of
    slot_range = jnp.arange(EXPERTS * CAP, dtype=jnp.int32)
    placed = destination.reshape(tokens_per_device, TOPK)[None, :, :] == slot_range[:, None, None]
    send_rows = jnp.dot(
        jnp.any(placed, axis=2).astype(jnp.bfloat16), normed, preferred_element_type=jnp.float32
    ).astype(jnp.bfloat16)
    split = FF // (expert_gate_up.shape[2] // 2)
    expert_rows = direct_dispatch(
        send_rows,
        split,
        jnp.concatenate([expert_gate_up, sibling_gate_up], axis=0),
        jnp.concatenate([expert_down, sibling_down], axis=0),
    )
    mixing = jnp.sum(jnp.where(placed, route_weight[None, :, :], 0.0), axis=2).T
    experts_sum = jnp.dot(
        mixing,
        expert_rows.astype(jnp.float32),
        precision=lax.Precision.HIGHEST,
        preferred_element_type=jnp.float32,
    )
    layer_out = (residual + experts_sum).astype(jnp.bfloat16)
    return (attended, layer_out)


def solution(mesh):
    placed = (
        P(("tok", "pool"), None),
        P(("tok", "pool"), None),
        P(("tok", "pool"), None),
        P(("tok", "pool"), None, None),
        P("tok", None),
        P("tok", None),
        P("tok", None),
        P(),
        P(),
        P("tok", None, None),
        P("tok", None, None),
        P(("tok", "pool"), None),
        P(("tok", "pool"), None),
    )
    return jax.shard_map(
        body,
        mesh=mesh,
        in_specs=placed,
        out_specs=(P(("tok", "pool"), None), P(("tok", "pool"), None)),
        check_vma=False,
    )
```

```python
import jax
import jax.numpy as jnp
from jax import lax
from jax.experimental import pallas as pl
from jax.experimental.pallas import tpu as pltpu
from jax.sharding import PartitionSpec as P

QUERY_HEADS = 16
KEY_VALUE_HEADS = 8
HEAD_SIZE = 64
EXPERTS = 32
FF = 512
TOPK = 8
CAP = 32


score_scale = 0.015625
masked_filler = -1e30


def _attend_kernel(q_ref, kv_ref, mask_ref, out_ref):
    rows = q_ref.shape[0]
    shown = mask_ref[...] > 0.5
    visible = jnp.concatenate([shown, shown], axis=0)
    lane = lax.broadcasted_iota(jnp.int32, (rows, 128), 1)
    low_half = lane < HEAD_SIZE
    stats = jnp.zeros((rows, 128), jnp.float32)
    for h in range(KEY_VALUE_HEADS):
        q_tile = q_ref[:, h * 128:(h + 1) * 128].astype(jnp.float32)
        k_tile = kv_ref[:, (h // 2) * 128:(h // 2 + 1) * 128]
        v_start = KEY_VALUE_HEADS * HEAD_SIZE + (h // 2) * 128
        v_tile = kv_ref[:, v_start:v_start + 128]
        halves = []
        for g in range(2):
            q_half = jnp.where(low_half if g == 0 else ~low_half, q_tile, 0.0)
            if g != h % 2:
                q_half = pltpu.roll(q_half, HEAD_SIZE, 1)
            halves.append(q_half)
        q_pair = jnp.concatenate(halves, axis=0).astype(jnp.bfloat16)
        scores = lax.dot_general(
            q_pair, k_tile, (((1,), (1,)), ((), ())), preferred_element_type=jnp.float32
        ) * score_scale
        scores = jnp.where(visible, scores, masked_filler)
        highest = jnp.max(scores, axis=1, keepdims=True)
        weights = jnp.where(visible, jnp.exp(scores - highest), 0.0)
        total = jnp.sum(weights, axis=1, keepdims=True)
        acc = jnp.dot(weights.astype(jnp.bfloat16), v_tile, preferred_element_type=jnp.float32)
        out_tile = jnp.zeros((rows, 128), jnp.float32)
        for g in range(2):
            part = acc[g * rows:(g + 1) * rows]
            if g != h % 2:
                part = pltpu.roll(part, HEAD_SIZE, 1)
            out_tile = jnp.where(low_half if g == 0 else ~low_half, part, out_tile)
            j = 2 * h + g
            stats = jnp.where(lane == j, highest[g * rows:(g + 1) * rows], stats)
            stats = jnp.where(lane == QUERY_HEADS + j, total[g * rows:(g + 1) * rows], stats)
        out_ref[:, h * 128:(h + 1) * 128] = out_tile
    out_ref[:, QUERY_HEADS * HEAD_SIZE:QUERY_HEADS * HEAD_SIZE + 128] = stats


def attend_partial(q_block, kv, mask):
    rows = q_block.shape[0]
    return pl.pallas_call(
        _attend_kernel,
        out_shape=jax.ShapeDtypeStruct((rows, QUERY_HEADS * HEAD_SIZE + 128), jnp.float32),
    )(q_block, kv, mask)


def pair_ffn(rows_in, gate_up_pair, down_pair):
    hidden_units = gate_up_pair.shape[2] // 2
    total = None
    for part in range(gate_up_pair.shape[0]):
        gate_up = jnp.dot(rows_in, gate_up_pair[part], preferred_element_type=jnp.float32)
        inner = (jax.nn.silu(gate_up[:, :hidden_units]) * gate_up[:, hidden_units:]).astype(
            jnp.bfloat16
        )
        produced = jnp.dot(inner, down_pair[part], preferred_element_type=jnp.float32).astype(
            jnp.bfloat16
        ).astype(jnp.float32)
        total = produced if total is None else total + produced
    return total.astype(jnp.bfloat16)


def direct_dispatch(send_rows, split, expert_gate_up, expert_down):
    width = send_rows.shape[1]
    gate_up_pair, down_pair = expert_gate_up, expert_down
    unit_rows = send_rows.reshape(EXPERTS * split, CAP // split, width)
    arrived = lax.all_to_all(unit_rows, "tok", split_axis=0, concat_axis=0, tiled=True)
    produced = pair_ffn(arrived.reshape(-1, width), gate_up_pair, down_pair)
    returned = lax.all_to_all(
        produced.reshape(EXPERTS * split, CAP // split, width),
        "tok",
        split_axis=0,
        concat_axis=0,
        tiled=True,
    )
    return returned.reshape(EXPERTS * CAP, width)


def body(
    stream,
    queries,
    fresh_kv,
    cache_block_pool,
    block_table,
    cached_len,
    request_ids,
    output_weight,
    norm_gain,
    expert_gate_up,
    expert_down,
    routes,
    route_weight,
):
    tokens_per_device = stream.shape[0]
    tok_size = lax.axis_size("tok")
    sibling = [(t, t ^ 1) for t in range(tok_size)]
    sibling_gate_up = lax.ppermute(expert_gate_up, "tok", sibling)
    sibling_down = lax.ppermute(expert_down, "tok", sibling)
    kv_width = KEY_VALUE_HEADS * HEAD_SIZE
    pool_size = lax.axis_size("pool")
    pool_idx = lax.axis_index("pool")
    segments = request_ids[0]
    lengths = cached_len[0]
    table = block_table[0]
    list_len = table.shape[0]
    pool_blocks = cache_block_pool.shape[0]
    block_len = cache_block_pool.shape[1]
    request_range = jnp.arange(lengths.shape[0], dtype=jnp.int32)
    row_len = jnp.sum(
        jnp.where(segments[:, None] == request_range[None, :], lengths[None, :], 0), axis=1
    )
    local_slots = pool_idx * pool_blocks + jnp.arange(pool_blocks, dtype=jnp.int32)
    slot_block = (
        jnp.sum(
            jnp.where(
                table[None, :] == local_slots[:, None],
                jnp.arange(list_len, dtype=jnp.int32)[None, :] + 1,
                0,
            ),
            axis=1,
        )
        - 1
    )
    offsets = jnp.arange(block_len, dtype=jnp.int32)
    cache_pos = (slot_block[:, None] * block_len + offsets[None, :]).reshape(-1)
    cache_listed = jnp.repeat(slot_block >= 0, block_len)
    shifts = range(pool_size)
    fresh_order = pool_idx * tokens_per_device + jnp.arange(tokens_per_device, dtype=jnp.int32)
    fresh_seg = lax.dynamic_slice_in_dim(segments, pool_idx * tokens_per_device, tokens_per_device)
    key_value_pairs = jnp.concatenate(
        [cache_block_pool.reshape(pool_blocks * block_len, 2 * kv_width), fresh_kv], axis=0
    )

    def attend_block(query_block, source):
        first = source * tokens_per_device
        query_order = first + jnp.arange(tokens_per_device, dtype=jnp.int32)
        query_seg = lax.dynamic_slice_in_dim(segments, first, tokens_per_device)
        query_len = lax.dynamic_slice_in_dim(row_len, first, tokens_per_device)
        cache_visible = cache_listed[None, :] & (cache_pos[None, :] < query_len[:, None])
        fresh_visible = (fresh_seg[None, :] == query_seg[:, None]) & (
            fresh_order[None, :] <= query_order[:, None]
        )
        visible = jnp.concatenate([cache_visible, fresh_visible], axis=1)
        return attend_partial(query_block, key_value_pairs, visible.astype(jnp.float32))

    query_blocks = [queries] + [
        lax.ppermute(
            queries, "pool", [(i, (i + shift) % pool_size) for i in range(pool_size)]
        )
        for shift in shifts[1:]
    ]
    partials = [None] * pool_size
    for shift in list(shifts[1:]) + [0]:
        partial = attend_block(query_blocks[shift], (pool_idx - shift) % pool_size)
        if shift:
            partial = lax.ppermute(
                partial, "pool", [(i, (i - shift) % pool_size) for i in range(pool_size)]
            )
        partials[shift] = partial
    gathered = jnp.stack(partials)
    acc_width = QUERY_HEADS * HEAD_SIZE
    part_max = gathered[:, :, acc_width : acc_width + QUERY_HEADS]
    part_sum = gathered[:, :, acc_width + QUERY_HEADS : acc_width + 2 * QUERY_HEADS]
    running = jnp.max(part_max, axis=0)
    rescale = jnp.exp(part_max - running[None])
    denominator = jnp.sum(part_sum * rescale, axis=0)
    spread = (
        jnp.arange(acc_width, dtype=jnp.int32)[None, :] // HEAD_SIZE
        == jnp.arange(QUERY_HEADS, dtype=jnp.int32)[:, None]
    ).astype(jnp.float32)

    def widen(per_head):
        return jnp.dot(
            per_head, spread, precision=lax.Precision.HIGHEST, preferred_element_type=jnp.float32
        )

    summed = sum(gathered[p, :, :acc_width] * widen(rescale[p]) for p in range(pool_size))
    denominator = widen(denominator)
    context = summed / denominator
    attended = context.reshape(tokens_per_device, QUERY_HEADS * HEAD_SIZE).astype(jnp.bfloat16)
    residual = stream.astype(jnp.float32) + jnp.dot(
        attended, output_weight, preferred_element_type=jnp.float32
    )
    meansq = jnp.mean(residual * residual, axis=-1, keepdims=True)
    normed = (residual * lax.rsqrt(meansq + 1e-06) * norm_gain).astype(jnp.bfloat16)
    flat_routes = routes.reshape(-1)
    onehot = (flat_routes[:, None] == jnp.arange(EXPERTS, dtype=jnp.int32)[None, :]).astype(
        jnp.int32
    )
    earlier = jnp.cumsum(onehot, axis=0) - onehot
    slot_of = jnp.sum(earlier * onehot, axis=1)
    destination = flat_routes * CAP + slot_of
    slot_range = jnp.arange(EXPERTS * CAP, dtype=jnp.int32)
    placed = destination.reshape(tokens_per_device, TOPK)[None, :, :] == slot_range[:, None, None]
    send_rows = jnp.dot(
        jnp.any(placed, axis=2).astype(jnp.bfloat16), normed, preferred_element_type=jnp.float32
    ).astype(jnp.bfloat16)
    split = FF // (expert_gate_up.shape[2] // 2)
    expert_rows = direct_dispatch(
        send_rows,
        split,
        jnp.concatenate([expert_gate_up, sibling_gate_up], axis=0),
        jnp.concatenate([expert_down, sibling_down], axis=0),
    )
    mixing = jnp.sum(jnp.where(placed, route_weight[None, :, :], 0.0), axis=2).T
    experts_sum = jnp.dot(
        mixing,
        expert_rows.astype(jnp.float32),
        precision=lax.Precision.HIGHEST,
        preferred_element_type=jnp.float32,
    )
    layer_out = (residual + experts_sum).astype(jnp.bfloat16)
    return (attended, layer_out)


def solution(mesh):
    placed = (
        P(("tok", "pool"), None),
        P(("tok", "pool"), None),
        P(("tok", "pool"), None),
        P(("tok", "pool"), None, None),
        P("tok", None),
        P("tok", None),
        P("tok", None),
        P(),
        P(),
        P("tok", None, None),
        P("tok", None, None),
        P(("tok", "pool"), None),
        P(("tok", "pool"), None),
    )
    return jax.shard_map(
        body,
        mesh=mesh,
        in_specs=placed,
        out_specs=(P(("tok", "pool"), None), P(("tok", "pool"), None)),
        check_vma=False,
    )
```

```python
import jax
import jax.numpy as jnp
from jax import lax
from jax.experimental import pallas as pl
from jax.experimental.pallas import tpu as pltpu
from jax.sharding import PartitionSpec as P

QUERY_HEADS = 16
KEY_VALUE_HEADS = 8
HEAD_SIZE = 64
EXPERTS = 32
FF = 512
TOPK = 8
CAP = 32
FRESH_BASE = 1 << 20


score_scale = 0.015625
masked_filler = -1e30


def _attend_kernel(
    source_ref, q_ref, kv_ref, query_len_ref, query_seg_ref, key_pos_ref, key_seg_ref, out_ref
):
    rows = q_ref.shape[0]
    first = pl.multiple_of(source_ref[0] * rows, rows)
    query_len = query_len_ref[pl.ds(first, rows), :]
    query_seg = query_seg_ref[pl.ds(first, rows), :]
    query_order = first + lax.broadcasted_iota(jnp.int32, (rows, 1), 0)
    key_pos = key_pos_ref[...]
    shown = (key_pos < query_len) | (
        (key_seg_ref[...] == query_seg) & (key_pos - FRESH_BASE <= query_order)
    )
    visible = jnp.concatenate([shown, shown], axis=0)
    lane = lax.broadcasted_iota(jnp.int32, (rows, 128), 1)
    low_half = lane < HEAD_SIZE
    stats = jnp.zeros((rows, 128), jnp.float32)
    for h in range(KEY_VALUE_HEADS):
        q_tile = q_ref[:, h * 128:(h + 1) * 128].astype(jnp.float32)
        k_tile = kv_ref[:, (h // 2) * 128:(h // 2 + 1) * 128]
        v_start = KEY_VALUE_HEADS * HEAD_SIZE + (h // 2) * 128
        v_tile = kv_ref[:, v_start:v_start + 128]
        halves = []
        for g in range(2):
            q_half = jnp.where(low_half if g == 0 else ~low_half, q_tile, 0.0)
            if g != h % 2:
                q_half = pltpu.roll(q_half, HEAD_SIZE, 1)
            halves.append(q_half)
        q_pair = jnp.concatenate(halves, axis=0).astype(jnp.bfloat16)
        scores = lax.dot_general(
            q_pair, k_tile, (((1,), (1,)), ((), ())), preferred_element_type=jnp.float32
        ) * score_scale
        scores = jnp.where(visible, scores, masked_filler)
        highest = jnp.max(scores, axis=1, keepdims=True)
        weights = jnp.where(visible, jnp.exp(scores - highest), 0.0)
        total = jnp.sum(weights, axis=1, keepdims=True)
        acc = jnp.dot(weights.astype(jnp.bfloat16), v_tile, preferred_element_type=jnp.float32)
        out_tile = jnp.zeros((rows, 128), jnp.float32)
        for g in range(2):
            part = acc[g * rows:(g + 1) * rows]
            if g != h % 2:
                part = pltpu.roll(part, HEAD_SIZE, 1)
            out_tile = jnp.where(low_half if g == 0 else ~low_half, part, out_tile)
            j = 2 * h + g
            stats = jnp.where(lane == j, highest[g * rows:(g + 1) * rows], stats)
            stats = jnp.where(lane == QUERY_HEADS + j, total[g * rows:(g + 1) * rows], stats)
        out_ref[:, h * 128:(h + 1) * 128] = out_tile
    out_ref[:, QUERY_HEADS * HEAD_SIZE:QUERY_HEADS * HEAD_SIZE + 128] = stats


def attend_partial(source, q_block, kv, query_len, query_seg, key_pos, key_seg):
    rows = q_block.shape[0]
    whole = lambda shape: pl.BlockSpec(shape, lambda i, s: (0,) * len(shape))
    operands = (q_block, kv, query_len, query_seg, key_pos, key_seg)
    return pl.pallas_call(
        _attend_kernel,
        out_shape=jax.ShapeDtypeStruct((rows, QUERY_HEADS * HEAD_SIZE + 128), jnp.float32),
        grid_spec=pltpu.PrefetchScalarGridSpec(
            num_scalar_prefetch=1,
            grid=(1,),
            in_specs=[whole(x.shape) for x in operands],
            out_specs=whole((rows, QUERY_HEADS * HEAD_SIZE + 128)),
        ),
    )(jnp.reshape(source, (1,)).astype(jnp.int32), *operands)


def pair_ffn(rows_in, gate_up_pair, down_pair):
    hidden_units = gate_up_pair.shape[2] // 2
    total = None
    for part in range(gate_up_pair.shape[0]):
        gate_up = jnp.dot(rows_in, gate_up_pair[part], preferred_element_type=jnp.float32)
        inner = (jax.nn.silu(gate_up[:, :hidden_units]) * gate_up[:, hidden_units:]).astype(
            jnp.bfloat16
        )
        produced = jnp.dot(inner, down_pair[part], preferred_element_type=jnp.float32).astype(
            jnp.bfloat16
        ).astype(jnp.float32)
        total = produced if total is None else total + produced
    return total.astype(jnp.bfloat16)


def direct_dispatch(send_rows, split, expert_gate_up, expert_down):
    width = send_rows.shape[1]
    gate_up_pair, down_pair = expert_gate_up, expert_down
    unit_rows = send_rows.reshape(EXPERTS * split, CAP // split, width)
    arrived = lax.all_to_all(unit_rows, "tok", split_axis=0, concat_axis=0, tiled=True)
    produced = pair_ffn(arrived.reshape(-1, width), gate_up_pair, down_pair)
    returned = lax.all_to_all(
        produced.reshape(EXPERTS * split, CAP // split, width),
        "tok",
        split_axis=0,
        concat_axis=0,
        tiled=True,
    )
    return returned.reshape(EXPERTS * CAP, width)


def body(
    stream,
    queries,
    fresh_kv,
    cache_block_pool,
    block_table,
    cached_len,
    request_ids,
    output_weight,
    norm_gain,
    expert_gate_up,
    expert_down,
    routes,
    route_weight,
):
    tokens_per_device = stream.shape[0]
    tok_size = lax.axis_size("tok")
    sibling = [(t, t ^ 1) for t in range(tok_size)]
    sibling_gate_up = lax.ppermute(expert_gate_up, "tok", sibling)
    sibling_down = lax.ppermute(expert_down, "tok", sibling)
    kv_width = KEY_VALUE_HEADS * HEAD_SIZE
    pool_size = lax.axis_size("pool")
    pool_idx = lax.axis_index("pool")
    segments = request_ids[0]
    lengths = cached_len[0]
    table = block_table[0]
    list_len = table.shape[0]
    pool_blocks = cache_block_pool.shape[0]
    block_len = cache_block_pool.shape[1]
    request_range = jnp.arange(lengths.shape[0], dtype=jnp.int32)
    row_len = jnp.sum(
        jnp.where(segments[:, None] == request_range[None, :], lengths[None, :], 0), axis=1
    )
    local_slots = pool_idx * pool_blocks + jnp.arange(pool_blocks, dtype=jnp.int32)
    slot_block = (
        jnp.sum(
            jnp.where(
                table[None, :] == local_slots[:, None],
                jnp.arange(list_len, dtype=jnp.int32)[None, :] + 1,
                0,
            ),
            axis=1,
        )
        - 1
    )
    offsets = jnp.arange(block_len, dtype=jnp.int32)
    cache_pos = (slot_block[:, None] * block_len + offsets[None, :]).reshape(-1)
    cache_listed = jnp.repeat(slot_block >= 0, block_len)
    shifts = range(pool_size)
    fresh_order = pool_idx * tokens_per_device + jnp.arange(tokens_per_device, dtype=jnp.int32)
    fresh_seg = lax.dynamic_slice_in_dim(segments, pool_idx * tokens_per_device, tokens_per_device)
    key_value_pairs = jnp.concatenate(
        [cache_block_pool.reshape(pool_blocks * block_len, 2 * kv_width), fresh_kv], axis=0
    )

    unlisted = jnp.int32(1 << 30)
    key_pos = jnp.concatenate(
        [jnp.where(cache_listed, cache_pos, unlisted), FRESH_BASE + fresh_order]
    ).reshape(1, -1)
    key_seg = jnp.concatenate(
        [jnp.full((pool_blocks * block_len,), -1, jnp.int32), fresh_seg]
    ).reshape(1, -1)
    query_len_all = row_len.reshape(-1, 1)
    query_seg_all = segments.reshape(-1, 1)

    def attend_block(query_block, source):
        return attend_partial(
            source, query_block, key_value_pairs, query_len_all, query_seg_all, key_pos, key_seg
        )

    query_blocks = [queries] + [
        lax.ppermute(
            queries, "pool", [(i, (i + shift) % pool_size) for i in range(pool_size)]
        )
        for shift in shifts[1:]
    ]
    partials = [None] * pool_size
    for shift in list(shifts[1:]) + [0]:
        partial = attend_block(query_blocks[shift], (pool_idx - shift) % pool_size)
        if shift:
            partial = lax.ppermute(
                partial, "pool", [(i, (i - shift) % pool_size) for i in range(pool_size)]
            )
        partials[shift] = partial
    gathered = jnp.stack(partials)
    acc_width = QUERY_HEADS * HEAD_SIZE
    part_max = gathered[:, :, acc_width : acc_width + QUERY_HEADS]
    part_sum = gathered[:, :, acc_width + QUERY_HEADS : acc_width + 2 * QUERY_HEADS]
    running = jnp.max(part_max, axis=0)
    rescale = jnp.exp(part_max - running[None])
    denominator = jnp.sum(part_sum * rescale, axis=0)
    spread = (
        jnp.arange(acc_width, dtype=jnp.int32)[None, :] // HEAD_SIZE
        == jnp.arange(QUERY_HEADS, dtype=jnp.int32)[:, None]
    ).astype(jnp.float32)

    def widen(per_head):
        return jnp.dot(
            per_head, spread, precision=lax.Precision.HIGHEST, preferred_element_type=jnp.float32
        )

    summed = sum(gathered[p, :, :acc_width] * widen(rescale[p]) for p in range(pool_size))
    denominator = widen(denominator)
    context = summed / denominator
    attended = context.reshape(tokens_per_device, QUERY_HEADS * HEAD_SIZE).astype(jnp.bfloat16)
    residual = stream.astype(jnp.float32) + jnp.dot(
        attended, output_weight, preferred_element_type=jnp.float32
    )
    meansq = jnp.mean(residual * residual, axis=-1, keepdims=True)
    normed = (residual * lax.rsqrt(meansq + 1e-06) * norm_gain).astype(jnp.bfloat16)
    flat_routes = routes.reshape(-1)
    onehot = (flat_routes[:, None] == jnp.arange(EXPERTS, dtype=jnp.int32)[None, :]).astype(
        jnp.int32
    )
    earlier = jnp.cumsum(onehot, axis=0) - onehot
    slot_of = jnp.sum(earlier * onehot, axis=1)
    destination = flat_routes * CAP + slot_of
    slot_range = jnp.arange(EXPERTS * CAP, dtype=jnp.int32)
    placed = destination.reshape(tokens_per_device, TOPK)[None, :, :] == slot_range[:, None, None]
    send_rows = jnp.dot(
        jnp.any(placed, axis=2).astype(jnp.bfloat16), normed, preferred_element_type=jnp.float32
    ).astype(jnp.bfloat16)
    split = FF // (expert_gate_up.shape[2] // 2)
    expert_rows = direct_dispatch(
        send_rows,
        split,
        jnp.concatenate([expert_gate_up, sibling_gate_up], axis=0),
        jnp.concatenate([expert_down, sibling_down], axis=0),
    )
    mixing = jnp.sum(jnp.where(placed, route_weight[None, :, :], 0.0), axis=2).T
    experts_sum = jnp.dot(
        mixing,
        expert_rows.astype(jnp.float32),
        precision=lax.Precision.HIGHEST,
        preferred_element_type=jnp.float32,
    )
    layer_out = (residual + experts_sum).astype(jnp.bfloat16)
    return (attended, layer_out)


def solution(mesh):
    placed = (
        P(("tok", "pool"), None),
        P(("tok", "pool"), None),
        P(("tok", "pool"), None),
        P(("tok", "pool"), None, None),
        P("tok", None),
        P("tok", None),
        P("tok", None),
        P(),
        P(),
        P("tok", None, None),
        P("tok", None, None),
        P(("tok", "pool"), None),
        P(("tok", "pool"), None),
    )
    return jax.shard_map(
        body,
        mesh=mesh,
        in_specs=placed,
        out_specs=(P(("tok", "pool"), None), P(("tok", "pool"), None)),
        check_vma=False,
    )
```

```python
import jax
import jax.numpy as jnp
from jax import lax
from jax.experimental import pallas as pl
from jax.experimental.pallas import tpu as pltpu
from jax.sharding import PartitionSpec as P

QUERY_HEADS = 16
KEY_VALUE_HEADS = 8
HEAD_SIZE = 64
EXPERTS = 32
FF = 512
TOPK = 8
CAP = 32
FRESH_BASE = 1 << 20


score_scale = 0.015625
masked_filler = -1e30


def _attend_kernel(
    source_ref, q_ref, kv_ref, query_len_ref, query_seg_ref, key_pos_ref, key_seg_ref, out_ref
):
    rows = q_ref.shape[0]
    first = pl.multiple_of(source_ref[0] * rows, rows)
    query_len = query_len_ref[pl.ds(first, rows), :]
    query_seg = query_seg_ref[pl.ds(first, rows), :]
    query_order = first + lax.broadcasted_iota(jnp.int32, (rows, 1), 0)
    key_pos = key_pos_ref[...]
    shown = (key_pos < query_len) | (
        (key_seg_ref[...] == query_seg) & (key_pos - FRESH_BASE <= query_order)
    )
    lane = lax.broadcasted_iota(jnp.int32, (rows, 128), 1)
    low_half = lane < HEAD_SIZE
    stats = jnp.zeros((rows, 128), jnp.float32)
    heads_per_tile = 128 // HEAD_SIZE
    visible = jnp.concatenate([shown] * (2 * heads_per_tile), axis=0)
    for t in range(KEY_VALUE_HEADS // heads_per_tile):
        k_tile = kv_ref[:, t * 128:(t + 1) * 128]
        v_start = KEY_VALUE_HEADS * HEAD_SIZE + t * 128
        v_tile = kv_ref[:, v_start:v_start + 128]
        pieces = []
        for h in range(t * heads_per_tile, (t + 1) * heads_per_tile):
            q_tile = q_ref[:, h * 128:(h + 1) * 128].astype(jnp.float32)
            for g in range(2):
                q_half = jnp.where(low_half if g == 0 else ~low_half, q_tile, 0.0)
                if g != h % 2:
                    q_half = pltpu.roll(q_half, HEAD_SIZE, 1)
                pieces.append(q_half)
        q_stack = jnp.concatenate(pieces, axis=0).astype(jnp.bfloat16)
        scores = lax.dot_general(
            q_stack, k_tile, (((1,), (1,)), ((), ())), preferred_element_type=jnp.float32
        ) * score_scale
        scores = jnp.where(visible, scores, masked_filler)
        highest = jnp.max(scores, axis=1, keepdims=True)
        weights = jnp.where(visible, jnp.exp(scores - highest), 0.0)
        total = jnp.sum(weights, axis=1, keepdims=True)
        acc = jnp.dot(weights.astype(jnp.bfloat16), v_tile, preferred_element_type=jnp.float32)
        for local, h in enumerate(range(t * heads_per_tile, (t + 1) * heads_per_tile)):
            out_tile = jnp.zeros((rows, 128), jnp.float32)
            for g in range(2):
                at = (2 * local + g) * rows
                part = acc[at:at + rows]
                if g != h % 2:
                    part = pltpu.roll(part, HEAD_SIZE, 1)
                out_tile = jnp.where(low_half if g == 0 else ~low_half, part, out_tile)
                j = 2 * h + g
                stats = jnp.where(lane == j, highest[at:at + rows], stats)
                stats = jnp.where(lane == QUERY_HEADS + j, total[at:at + rows], stats)
            out_ref[:, h * 128:(h + 1) * 128] = out_tile
    out_ref[:, QUERY_HEADS * HEAD_SIZE:QUERY_HEADS * HEAD_SIZE + 128] = stats


def attend_partial(source, q_block, kv, query_len, query_seg, key_pos, key_seg):
    rows = q_block.shape[0]
    whole = lambda shape: pl.BlockSpec(shape, lambda i, s: (0,) * len(shape))
    operands = (q_block, kv, query_len, query_seg, key_pos, key_seg)
    return pl.pallas_call(
        _attend_kernel,
        out_shape=jax.ShapeDtypeStruct((rows, QUERY_HEADS * HEAD_SIZE + 128), jnp.float32),
        grid_spec=pltpu.PrefetchScalarGridSpec(
            num_scalar_prefetch=1,
            grid=(1,),
            in_specs=[whole(x.shape) for x in operands],
            out_specs=whole((rows, QUERY_HEADS * HEAD_SIZE + 128)),
        ),
    )(jnp.reshape(source, (1,)).astype(jnp.int32), *operands)


def pair_ffn(rows_in, gate_up_pair, down_pair):
    hidden_units = gate_up_pair.shape[2] // 2
    total = None
    for part in range(gate_up_pair.shape[0]):
        gate_up = jnp.dot(rows_in, gate_up_pair[part], preferred_element_type=jnp.float32)
        inner = (jax.nn.silu(gate_up[:, :hidden_units]) * gate_up[:, hidden_units:]).astype(
            jnp.bfloat16
        )
        produced = jnp.dot(inner, down_pair[part], preferred_element_type=jnp.float32).astype(
            jnp.bfloat16
        ).astype(jnp.float32)
        total = produced if total is None else total + produced
    return total.astype(jnp.bfloat16)


def direct_dispatch(send_rows, split, expert_gate_up, expert_down):
    width = send_rows.shape[1]
    gate_up_pair, down_pair = expert_gate_up, expert_down
    unit_rows = send_rows.reshape(EXPERTS * split, CAP // split, width)
    arrived = lax.all_to_all(unit_rows, "tok", split_axis=0, concat_axis=0, tiled=True)
    produced = pair_ffn(arrived.reshape(-1, width), gate_up_pair, down_pair)
    returned = lax.all_to_all(
        produced.reshape(EXPERTS * split, CAP // split, width),
        "tok",
        split_axis=0,
        concat_axis=0,
        tiled=True,
    )
    return returned.reshape(EXPERTS * CAP, width)


def body(
    stream,
    queries,
    fresh_kv,
    cache_block_pool,
    block_table,
    cached_len,
    request_ids,
    output_weight,
    norm_gain,
    expert_gate_up,
    expert_down,
    routes,
    route_weight,
):
    tokens_per_device = stream.shape[0]
    tok_size = lax.axis_size("tok")
    sibling = [(t, t ^ 1) for t in range(tok_size)]
    sibling_gate_up = lax.ppermute(expert_gate_up, "tok", sibling)
    sibling_down = lax.ppermute(expert_down, "tok", sibling)
    kv_width = KEY_VALUE_HEADS * HEAD_SIZE
    pool_size = lax.axis_size("pool")
    pool_idx = lax.axis_index("pool")
    segments = request_ids[0]
    lengths = cached_len[0]
    table = block_table[0]
    list_len = table.shape[0]
    pool_blocks = cache_block_pool.shape[0]
    block_len = cache_block_pool.shape[1]
    request_range = jnp.arange(lengths.shape[0], dtype=jnp.int32)
    row_len = jnp.sum(
        jnp.where(segments[:, None] == request_range[None, :], lengths[None, :], 0), axis=1
    )
    local_slots = pool_idx * pool_blocks + jnp.arange(pool_blocks, dtype=jnp.int32)
    slot_block = (
        jnp.sum(
            jnp.where(
                table[None, :] == local_slots[:, None],
                jnp.arange(list_len, dtype=jnp.int32)[None, :] + 1,
                0,
            ),
            axis=1,
        )
        - 1
    )
    offsets = jnp.arange(block_len, dtype=jnp.int32)
    cache_pos = (slot_block[:, None] * block_len + offsets[None, :]).reshape(-1)
    cache_listed = jnp.repeat(slot_block >= 0, block_len)
    shifts = range(pool_size)
    fresh_order = pool_idx * tokens_per_device + jnp.arange(tokens_per_device, dtype=jnp.int32)
    fresh_seg = lax.dynamic_slice_in_dim(segments, pool_idx * tokens_per_device, tokens_per_device)
    key_value_pairs = jnp.concatenate(
        [cache_block_pool.reshape(pool_blocks * block_len, 2 * kv_width), fresh_kv], axis=0
    )

    unlisted = jnp.int32(1 << 30)
    key_pos = jnp.concatenate(
        [jnp.where(cache_listed, cache_pos, unlisted), FRESH_BASE + fresh_order]
    ).reshape(1, -1)
    key_seg = jnp.concatenate(
        [jnp.full((pool_blocks * block_len,), -1, jnp.int32), fresh_seg]
    ).reshape(1, -1)
    query_len_all = row_len.reshape(-1, 1)
    query_seg_all = segments.reshape(-1, 1)

    def attend_block(query_block, source):
        return attend_partial(
            source, query_block, key_value_pairs, query_len_all, query_seg_all, key_pos, key_seg
        )

    query_blocks = [queries] + [
        lax.ppermute(
            queries, "pool", [(i, (i + shift) % pool_size) for i in range(pool_size)]
        )
        for shift in shifts[1:]
    ]
    partials = [None] * pool_size
    for shift in list(shifts[1:]) + [0]:
        partial = attend_block(query_blocks[shift], (pool_idx - shift) % pool_size)
        if shift:
            partial = lax.ppermute(
                partial, "pool", [(i, (i - shift) % pool_size) for i in range(pool_size)]
            )
        partials[shift] = partial
    gathered = jnp.stack(partials)
    acc_width = QUERY_HEADS * HEAD_SIZE
    part_max = gathered[:, :, acc_width : acc_width + QUERY_HEADS]
    part_sum = gathered[:, :, acc_width + QUERY_HEADS : acc_width + 2 * QUERY_HEADS]
    running = jnp.max(part_max, axis=0)
    rescale = jnp.exp(part_max - running[None])
    denominator = jnp.sum(part_sum * rescale, axis=0)
    spread = (
        jnp.arange(acc_width, dtype=jnp.int32)[None, :] // HEAD_SIZE
        == jnp.arange(QUERY_HEADS, dtype=jnp.int32)[:, None]
    ).astype(jnp.float32)

    def widen(per_head):
        return jnp.dot(
            per_head, spread, precision=lax.Precision.HIGHEST, preferred_element_type=jnp.float32
        )

    summed = sum(gathered[p, :, :acc_width] * widen(rescale[p]) for p in range(pool_size))
    denominator = widen(denominator)
    context = summed / denominator
    attended = context.reshape(tokens_per_device, QUERY_HEADS * HEAD_SIZE).astype(jnp.bfloat16)
    residual = stream.astype(jnp.float32) + jnp.dot(
        attended, output_weight, preferred_element_type=jnp.float32
    )
    meansq = jnp.mean(residual * residual, axis=-1, keepdims=True)
    normed = (residual * lax.rsqrt(meansq + 1e-06) * norm_gain).astype(jnp.bfloat16)
    flat_routes = routes.reshape(-1)
    onehot = (flat_routes[:, None] == jnp.arange(EXPERTS, dtype=jnp.int32)[None, :]).astype(
        jnp.int32
    )
    earlier = jnp.cumsum(onehot, axis=0) - onehot
    slot_of = jnp.sum(earlier * onehot, axis=1)
    destination = flat_routes * CAP + slot_of
    slot_range = jnp.arange(EXPERTS * CAP, dtype=jnp.int32)
    placed = destination.reshape(tokens_per_device, TOPK)[None, :, :] == slot_range[:, None, None]
    send_rows = jnp.dot(
        jnp.any(placed, axis=2).astype(jnp.bfloat16), normed, preferred_element_type=jnp.float32
    ).astype(jnp.bfloat16)
    split = FF // (expert_gate_up.shape[2] // 2)
    expert_rows = direct_dispatch(
        send_rows,
        split,
        jnp.concatenate([expert_gate_up, sibling_gate_up], axis=0),
        jnp.concatenate([expert_down, sibling_down], axis=0),
    )
    mixing = jnp.sum(jnp.where(placed, route_weight[None, :, :], 0.0), axis=2).T
    experts_sum = jnp.dot(
        mixing,
        expert_rows.astype(jnp.float32),
        precision=lax.Precision.HIGHEST,
        preferred_element_type=jnp.float32,
    )
    layer_out = (residual + experts_sum).astype(jnp.bfloat16)
    return (attended, layer_out)


def solution(mesh):
    placed = (
        P(("tok", "pool"), None),
        P(("tok", "pool"), None),
        P(("tok", "pool"), None),
        P(("tok", "pool"), None, None),
        P("tok", None),
        P("tok", None),
        P("tok", None),
        P(),
        P(),
        P("tok", None, None),
        P("tok", None, None),
        P(("tok", "pool"), None),
        P(("tok", "pool"), None),
    )
    return jax.shard_map(
        body,
        mesh=mesh,
        in_specs=placed,
        out_specs=(P(("tok", "pool"), None), P(("tok", "pool"), None)),
        check_vma=False,
    )
```

```python
import jax
import jax.numpy as jnp
from jax import lax
from jax.experimental import pallas as pl
from jax.experimental.pallas import tpu as pltpu
from jax.sharding import PartitionSpec as P

QUERY_HEADS = 16
KEY_VALUE_HEADS = 8
HEAD_SIZE = 64
EXPERTS = 32
FF = 512
TOPK = 8
CAP = 32
FRESH_BASE = 1 << 20


score_scale = 0.015625
masked_filler = -1e30


def _attend_kernel(
    source_ref, q_ref, kv_ref, query_len_ref, query_seg_ref, key_pos_ref, key_seg_ref, out_ref
):
    rows = q_ref.shape[0]
    first = pl.multiple_of(source_ref[0] * rows, rows)
    query_len = query_len_ref[pl.ds(first, rows), :]
    query_seg = query_seg_ref[pl.ds(first, rows), :]
    query_order = first + lax.broadcasted_iota(jnp.int32, (rows, 1), 0)
    key_pos = key_pos_ref[...]
    shown = (key_pos < query_len) | (
        (key_seg_ref[...] == query_seg) & (key_pos - FRESH_BASE <= query_order)
    )
    lane = lax.broadcasted_iota(jnp.int32, (rows, 128), 1)
    low_half = lane < HEAD_SIZE
    stats = jnp.zeros((rows, 128), jnp.float32)
    heads_per_tile = 128 // HEAD_SIZE
    visible = jnp.concatenate([shown] * (2 * heads_per_tile), axis=0)
    for t in range(KEY_VALUE_HEADS // heads_per_tile):
        k_tile = kv_ref[:, t * 128:(t + 1) * 128]
        v_start = KEY_VALUE_HEADS * HEAD_SIZE + t * 128
        v_tile = kv_ref[:, v_start:v_start + 128]
        pieces = []
        for h in range(t * heads_per_tile, (t + 1) * heads_per_tile):
            q_tile = q_ref[:, h * 128:(h + 1) * 128].astype(jnp.float32)
            for g in range(2):
                q_half = jnp.where(low_half if g == 0 else ~low_half, q_tile, 0.0)
                if g != h % 2:
                    q_half = pltpu.roll(q_half, HEAD_SIZE, 1)
                pieces.append(q_half)
        q_stack = jnp.concatenate(pieces, axis=0).astype(jnp.bfloat16)
        scores = lax.dot_general(
            q_stack, k_tile, (((1,), (1,)), ((), ())), preferred_element_type=jnp.float32
        ) * score_scale
        scores = jnp.where(visible, scores, masked_filler)
        highest = jnp.max(scores, axis=1, keepdims=True)
        weights = jnp.where(visible, jnp.exp(scores - highest), 0.0)
        total = jnp.sum(weights, axis=1, keepdims=True)
        acc = jnp.dot(weights.astype(jnp.bfloat16), v_tile, preferred_element_type=jnp.float32)
        for local, h in enumerate(range(t * heads_per_tile, (t + 1) * heads_per_tile)):
            out_tile = jnp.zeros((rows, 128), jnp.float32)
            for g in range(2):
                at = (2 * local + g) * rows
                part = acc[at:at + rows]
                if g != h % 2:
                    part = pltpu.roll(part, HEAD_SIZE, 1)
                out_tile = jnp.where(low_half if g == 0 else ~low_half, part, out_tile)
                j = 2 * h + g
                stats = jnp.where(lane == j, highest[at:at + rows], stats)
                stats = jnp.where(lane == QUERY_HEADS + j, total[at:at + rows], stats)
            out_ref[:, h * 128:(h + 1) * 128] = out_tile
    out_ref[:, QUERY_HEADS * HEAD_SIZE:QUERY_HEADS * HEAD_SIZE + 128] = stats


def attend_partial(source, q_block, kv, query_len, query_seg, key_pos, key_seg):
    rows = q_block.shape[0]
    whole = lambda shape: pl.BlockSpec(shape, lambda i, s: (0,) * len(shape))
    operands = (q_block, kv, query_len, query_seg, key_pos, key_seg)
    return pl.pallas_call(
        _attend_kernel,
        out_shape=jax.ShapeDtypeStruct((rows, QUERY_HEADS * HEAD_SIZE + 128), jnp.float32),
        grid_spec=pltpu.PrefetchScalarGridSpec(
            num_scalar_prefetch=1,
            grid=(1,),
            in_specs=[whole(x.shape) for x in operands],
            out_specs=whole((rows, QUERY_HEADS * HEAD_SIZE + 128)),
        ),
    )(jnp.reshape(source, (1,)).astype(jnp.int32), *operands)


def pair_ffn(rows_in, gate_up_pair, down_pair):
    hidden_units = gate_up_pair.shape[2] // 2
    total = None
    for part in range(gate_up_pair.shape[0]):
        gate_up = jnp.dot(rows_in, gate_up_pair[part], preferred_element_type=jnp.float32)
        inner = (jax.nn.silu(gate_up[:, :hidden_units]) * gate_up[:, hidden_units:]).astype(
            jnp.bfloat16
        )
        produced = jnp.dot(inner, down_pair[part], preferred_element_type=jnp.float32).astype(
            jnp.bfloat16
        ).astype(jnp.float32)
        total = produced if total is None else total + produced
    return total.astype(jnp.bfloat16)


def direct_dispatch(send_rows, split, expert_gate_up, expert_down):
    width = send_rows.shape[1]
    gate_up_pair, down_pair = expert_gate_up, expert_down
    unit_rows = send_rows.reshape(EXPERTS * split, CAP // split, width)
    arrived = lax.all_to_all(unit_rows, "tok", split_axis=0, concat_axis=0, tiled=True)
    produced = pair_ffn(arrived.reshape(-1, width), gate_up_pair, down_pair)
    returned = lax.all_to_all(
        produced.reshape(EXPERTS * split, CAP // split, width),
        "tok",
        split_axis=0,
        concat_axis=0,
        tiled=True,
    )
    return returned.reshape(EXPERTS * CAP, width)


def body(
    stream,
    queries,
    fresh_kv,
    cache_block_pool,
    block_table,
    cached_len,
    request_ids,
    output_weight,
    norm_gain,
    expert_gate_up,
    expert_down,
    routes,
    route_weight,
):
    tokens_per_device = stream.shape[0]
    tok_size = lax.axis_size("tok")
    sibling = [(t, t ^ 1) for t in range(tok_size)]
    sibling_gate_up = lax.ppermute(expert_gate_up, "tok", sibling)
    sibling_down = lax.ppermute(expert_down, "tok", sibling)
    kv_width = KEY_VALUE_HEADS * HEAD_SIZE
    pool_size = lax.axis_size("pool")
    pool_idx = lax.axis_index("pool")
    segments = request_ids[0]
    lengths = cached_len[0]
    table = block_table[0]
    list_len = table.shape[0]
    pool_blocks = cache_block_pool.shape[0]
    block_len = cache_block_pool.shape[1]
    request_range = jnp.arange(lengths.shape[0], dtype=jnp.int32)
    row_len = jnp.sum(
        jnp.where(segments[:, None] == request_range[None, :], lengths[None, :], 0), axis=1
    )
    local_slots = pool_idx * pool_blocks + jnp.arange(pool_blocks, dtype=jnp.int32)
    slot_block = (
        jnp.sum(
            jnp.where(
                table[None, :] == local_slots[:, None],
                jnp.arange(list_len, dtype=jnp.int32)[None, :] + 1,
                0,
            ),
            axis=1,
        )
        - 1
    )
    offsets = jnp.arange(block_len, dtype=jnp.int32)
    cache_pos = (slot_block[:, None] * block_len + offsets[None, :]).reshape(-1)
    cache_listed = jnp.repeat(slot_block >= 0, block_len)
    shifts = range(pool_size)
    fresh_order = pool_idx * tokens_per_device + jnp.arange(tokens_per_device, dtype=jnp.int32)
    fresh_seg = lax.dynamic_slice_in_dim(segments, pool_idx * tokens_per_device, tokens_per_device)
    key_value_pairs = jnp.concatenate(
        [cache_block_pool.reshape(pool_blocks * block_len, 2 * kv_width), fresh_kv], axis=0
    )

    unlisted = jnp.int32(1 << 30)
    key_pos = jnp.concatenate(
        [jnp.where(cache_listed, cache_pos, unlisted), FRESH_BASE + fresh_order]
    ).reshape(1, -1)
    key_seg = jnp.concatenate(
        [jnp.full((pool_blocks * block_len,), -1, jnp.int32), fresh_seg]
    ).reshape(1, -1)
    query_len_all = row_len.reshape(-1, 1)
    query_seg_all = segments.reshape(-1, 1)

    def attend_block(query_block, source):
        return attend_partial(
            source, query_block, key_value_pairs, query_len_all, query_seg_all, key_pos, key_seg
        )

    query_blocks = [queries] + [
        lax.ppermute(
            queries, "pool", [(i, (i + shift) % pool_size) for i in range(pool_size)]
        )
        for shift in shifts[1:]
    ]
    partials = [None] * pool_size
    for shift in ring_order(pool_size):
        partial = attend_block(query_blocks[shift], (pool_idx - shift) % pool_size)
        if shift:
            partial = lax.ppermute(
                partial, "pool", [(i, (i - shift) % pool_size) for i in range(pool_size)]
            )
        partials[shift] = partial
    gathered = jnp.stack(partials)
    acc_width = QUERY_HEADS * HEAD_SIZE
    part_max = gathered[:, :, acc_width : acc_width + QUERY_HEADS]
    part_sum = gathered[:, :, acc_width + QUERY_HEADS : acc_width + 2 * QUERY_HEADS]
    running = jnp.max(part_max, axis=0)
    rescale = jnp.exp(part_max - running[None])
    denominator = jnp.sum(part_sum * rescale, axis=0)
    spread = (
        jnp.arange(acc_width, dtype=jnp.int32)[None, :] // HEAD_SIZE
        == jnp.arange(QUERY_HEADS, dtype=jnp.int32)[:, None]
    ).astype(jnp.float32)

    def widen(per_head):
        return jnp.dot(
            per_head, spread, precision=lax.Precision.HIGHEST, preferred_element_type=jnp.float32
        )

    summed = sum(gathered[p, :, :acc_width] * widen(rescale[p]) for p in range(pool_size))
    denominator = widen(denominator)
    context = summed / denominator
    attended = context.reshape(tokens_per_device, QUERY_HEADS * HEAD_SIZE).astype(jnp.bfloat16)
    residual = stream.astype(jnp.float32) + jnp.dot(
        attended, output_weight, preferred_element_type=jnp.float32
    )
    meansq = jnp.mean(residual * residual, axis=-1, keepdims=True)
    normed = (residual * lax.rsqrt(meansq + 1e-06) * norm_gain).astype(jnp.bfloat16)
    flat_routes = routes.reshape(-1)
    onehot = (flat_routes[:, None] == jnp.arange(EXPERTS, dtype=jnp.int32)[None, :]).astype(
        jnp.int32
    )
    earlier = jnp.cumsum(onehot, axis=0) - onehot
    slot_of = jnp.sum(earlier * onehot, axis=1)
    destination = flat_routes * CAP + slot_of
    slot_range = jnp.arange(EXPERTS * CAP, dtype=jnp.int32)
    placed = destination.reshape(tokens_per_device, TOPK)[None, :, :] == slot_range[:, None, None]
    send_rows = jnp.dot(
        jnp.any(placed, axis=2).astype(jnp.bfloat16), normed, preferred_element_type=jnp.float32
    ).astype(jnp.bfloat16)
    split = FF // (expert_gate_up.shape[2] // 2)
    expert_rows = direct_dispatch(
        send_rows,
        split,
        jnp.concatenate([expert_gate_up, sibling_gate_up], axis=0),
        jnp.concatenate([expert_down, sibling_down], axis=0),
    )
    mixing = jnp.sum(jnp.where(placed, route_weight[None, :, :], 0.0), axis=2).T
    experts_sum = jnp.dot(
        mixing,
        expert_rows.astype(jnp.float32),
        precision=lax.Precision.HIGHEST,
        preferred_element_type=jnp.float32,
    )
    layer_out = (residual + experts_sum).astype(jnp.bfloat16)
    return (attended, layer_out)


def ring_order(pool_size):
    farthest = pool_size // 2
    return [farthest] + [s for s in range(1, pool_size) if s != farthest] + [0]


def solution(mesh):
    placed = (
        P(("tok", "pool"), None),
        P(("tok", "pool"), None),
        P(("tok", "pool"), None),
        P(("tok", "pool"), None, None),
        P("tok", None),
        P("tok", None),
        P("tok", None),
        P(),
        P(),
        P("tok", None, None),
        P("tok", None, None),
        P(("tok", "pool"), None),
        P(("tok", "pool"), None),
    )
    return jax.shard_map(
        body,
        mesh=mesh,
        in_specs=placed,
        out_specs=(P(("tok", "pool"), None), P(("tok", "pool"), None)),
        check_vma=False,
    )
```

```python
import jax
import jax.numpy as jnp
from jax import lax
from jax.experimental import pallas as pl
from jax.experimental.pallas import tpu as pltpu
from jax.sharding import PartitionSpec as P

QUERY_HEADS = 16
KEY_VALUE_HEADS = 8
HEAD_SIZE = 64
EXPERTS = 32
FF = 512
TOPK = 8
CAP = 32
FRESH_BASE = 1 << 20


score_scale = 0.015625
masked_filler = -1e30


def _attend_kernel(
    source_ref, q_ref, kv_ref, query_len_ref, query_seg_ref, key_pos_ref, key_seg_ref, out_ref
):
    rows = q_ref.shape[0]
    first = pl.multiple_of(source_ref[0] * rows, rows)
    group = query_len_ref.shape[1]
    pick = lax.broadcasted_iota(jnp.int32, (rows, group), 1) == (
        first + lax.broadcasted_iota(jnp.int32, (rows, group), 0)
    )

    def column(row_ref):
        row = row_ref[...].astype(jnp.float32)
        return jnp.sum(jnp.where(pick, row, 0.0), axis=1, keepdims=True).astype(jnp.int32)

    query_len = column(query_len_ref)
    query_seg = column(query_seg_ref)
    query_order = first + lax.broadcasted_iota(jnp.int32, (rows, 1), 0)
    key_pos = key_pos_ref[...]
    shown = (key_pos < query_len) | (
        (key_seg_ref[...] == query_seg) & (key_pos - FRESH_BASE <= query_order)
    )
    lane = lax.broadcasted_iota(jnp.int32, (rows, 128), 1)
    low_half = lane < HEAD_SIZE
    stats = jnp.zeros((rows, 128), jnp.float32)
    heads_per_tile = 128 // HEAD_SIZE
    visible = jnp.concatenate([shown] * (2 * heads_per_tile), axis=0)
    for t in range(KEY_VALUE_HEADS // heads_per_tile):
        k_tile = kv_ref[:, t * 128:(t + 1) * 128]
        v_start = KEY_VALUE_HEADS * HEAD_SIZE + t * 128
        v_tile = kv_ref[:, v_start:v_start + 128]
        pieces = []
        for h in range(t * heads_per_tile, (t + 1) * heads_per_tile):
            q_tile = q_ref[:, h * 128:(h + 1) * 128].astype(jnp.float32)
            for g in range(2):
                q_half = jnp.where(low_half if g == 0 else ~low_half, q_tile, 0.0)
                if g != h % 2:
                    q_half = pltpu.roll(q_half, HEAD_SIZE, 1)
                pieces.append(q_half)
        q_stack = jnp.concatenate(pieces, axis=0).astype(jnp.bfloat16)
        scores = lax.dot_general(
            q_stack, k_tile, (((1,), (1,)), ((), ())), preferred_element_type=jnp.float32
        ) * score_scale
        scores = jnp.where(visible, scores, masked_filler)
        highest = jnp.max(scores, axis=1, keepdims=True)
        weights = jnp.where(visible, jnp.exp(scores - highest), 0.0)
        total = jnp.sum(weights, axis=1, keepdims=True)
        acc = jnp.dot(weights.astype(jnp.bfloat16), v_tile, preferred_element_type=jnp.float32)
        for local, h in enumerate(range(t * heads_per_tile, (t + 1) * heads_per_tile)):
            out_tile = jnp.zeros((rows, 128), jnp.float32)
            for g in range(2):
                at = (2 * local + g) * rows
                part = acc[at:at + rows]
                if g != h % 2:
                    part = pltpu.roll(part, HEAD_SIZE, 1)
                out_tile = jnp.where(low_half if g == 0 else ~low_half, part, out_tile)
                j = 2 * h + g
                stats = jnp.where(lane == j, highest[at:at + rows], stats)
                stats = jnp.where(lane == QUERY_HEADS + j, total[at:at + rows], stats)
            out_ref[:, h * 128:(h + 1) * 128] = out_tile
    out_ref[:, QUERY_HEADS * HEAD_SIZE:QUERY_HEADS * HEAD_SIZE + 128] = stats


def attend_partial(source, q_block, kv, query_len, query_seg, key_pos, key_seg):
    rows = q_block.shape[0]
    whole = lambda shape: pl.BlockSpec(shape, lambda i, s: (0,) * len(shape))
    operands = (q_block, kv, query_len, query_seg, key_pos, key_seg)
    return pl.pallas_call(
        _attend_kernel,
        out_shape=jax.ShapeDtypeStruct((rows, QUERY_HEADS * HEAD_SIZE + 128), jnp.float32),
        grid_spec=pltpu.PrefetchScalarGridSpec(
            num_scalar_prefetch=1,
            grid=(1,),
            in_specs=[whole(x.shape) for x in operands],
            out_specs=whole((rows, QUERY_HEADS * HEAD_SIZE + 128)),
        ),
    )(jnp.reshape(source, (1,)).astype(jnp.int32), *operands)


def pair_ffn(rows_in, gate_up_pair, down_pair):
    hidden_units = gate_up_pair.shape[2] // 2
    total = None
    for part in range(gate_up_pair.shape[0]):
        gate_up = jnp.dot(rows_in, gate_up_pair[part], preferred_element_type=jnp.float32)
        inner = (jax.nn.silu(gate_up[:, :hidden_units]) * gate_up[:, hidden_units:]).astype(
            jnp.bfloat16
        )
        produced = jnp.dot(inner, down_pair[part], preferred_element_type=jnp.float32).astype(
            jnp.bfloat16
        ).astype(jnp.float32)
        total = produced if total is None else total + produced
    return total.astype(jnp.bfloat16)


def direct_dispatch(send_rows, split, expert_gate_up, expert_down):
    width = send_rows.shape[1]
    gate_up_pair, down_pair = expert_gate_up, expert_down
    unit_rows = send_rows.reshape(EXPERTS * split, CAP // split, width)
    arrived = lax.all_to_all(unit_rows, "tok", split_axis=0, concat_axis=0, tiled=True)
    produced = pair_ffn(arrived.reshape(-1, width), gate_up_pair, down_pair)
    returned = lax.all_to_all(
        produced.reshape(EXPERTS * split, CAP // split, width),
        "tok",
        split_axis=0,
        concat_axis=0,
        tiled=True,
    )
    return returned.reshape(EXPERTS * CAP, width)


def body(
    stream,
    queries,
    fresh_kv,
    cache_block_pool,
    block_table,
    cached_len,
    request_ids,
    output_weight,
    norm_gain,
    expert_gate_up,
    expert_down,
    routes,
    route_weight,
):
    tokens_per_device = stream.shape[0]
    tok_size = lax.axis_size("tok")
    sibling = [(t, t ^ 1) for t in range(tok_size)]
    sibling_gate_up = lax.ppermute(expert_gate_up, "tok", sibling)
    sibling_down = lax.ppermute(expert_down, "tok", sibling)
    kv_width = KEY_VALUE_HEADS * HEAD_SIZE
    pool_size = lax.axis_size("pool")
    pool_idx = lax.axis_index("pool")
    segments = request_ids[0]
    lengths = cached_len[0]
    table = block_table[0]
    list_len = table.shape[0]
    pool_blocks = cache_block_pool.shape[0]
    block_len = cache_block_pool.shape[1]
    request_range = jnp.arange(lengths.shape[0], dtype=jnp.int32)
    row_len = jnp.sum(
        jnp.where(segments[:, None] == request_range[None, :], lengths[None, :], 0), axis=1
    )
    local_slots = pool_idx * pool_blocks + jnp.arange(pool_blocks, dtype=jnp.int32)
    slot_block = (
        jnp.sum(
            jnp.where(
                table[None, :] == local_slots[:, None],
                jnp.arange(list_len, dtype=jnp.int32)[None, :] + 1,
                0,
            ),
            axis=1,
        )
        - 1
    )
    offsets = jnp.arange(block_len, dtype=jnp.int32)
    cache_pos = (slot_block[:, None] * block_len + offsets[None, :]).reshape(-1)
    cache_listed = jnp.repeat(slot_block >= 0, block_len)
    shifts = range(pool_size)
    fresh_order = pool_idx * tokens_per_device + jnp.arange(tokens_per_device, dtype=jnp.int32)
    fresh_seg = lax.dynamic_slice_in_dim(segments, pool_idx * tokens_per_device, tokens_per_device)
    key_value_pairs = jnp.concatenate(
        [cache_block_pool.reshape(pool_blocks * block_len, 2 * kv_width), fresh_kv], axis=0
    )

    unlisted = jnp.int32(1 << 30)
    key_pos = jnp.concatenate(
        [jnp.where(cache_listed, cache_pos, unlisted), FRESH_BASE + fresh_order]
    ).reshape(1, -1)
    key_seg = jnp.concatenate(
        [jnp.full((pool_blocks * block_len,), -1, jnp.int32), fresh_seg]
    ).reshape(1, -1)
    query_len_all = jnp.sum(
        jnp.where(
            request_ids[:, :, None] == request_range[None, None, :], lengths[None, None, :], 0
        ),
        axis=2,
    )
    query_seg_all = request_ids

    def attend_block(query_block, source):
        return attend_partial(
            source, query_block, key_value_pairs, query_len_all, query_seg_all, key_pos, key_seg
        )

    query_blocks = [queries] + [
        lax.ppermute(
            queries, "pool", [(i, (i + shift) % pool_size) for i in range(pool_size)]
        )
        for shift in shifts[1:]
    ]
    partials = [None] * pool_size
    for shift in ring_order(pool_size):
        partial = attend_block(query_blocks[shift], (pool_idx - shift) % pool_size)
        if shift:
            partial = lax.ppermute(
                partial, "pool", [(i, (i - shift) % pool_size) for i in range(pool_size)]
            )
        partials[shift] = partial
    gathered = jnp.stack(partials)
    acc_width = QUERY_HEADS * HEAD_SIZE
    part_max = gathered[:, :, acc_width : acc_width + QUERY_HEADS]
    part_sum = gathered[:, :, acc_width + QUERY_HEADS : acc_width + 2 * QUERY_HEADS]
    running = jnp.max(part_max, axis=0)
    rescale = jnp.exp(part_max - running[None])
    denominator = jnp.sum(part_sum * rescale, axis=0)
    spread = (
        jnp.arange(acc_width, dtype=jnp.int32)[None, :] // HEAD_SIZE
        == jnp.arange(QUERY_HEADS, dtype=jnp.int32)[:, None]
    ).astype(jnp.float32)

    def widen(per_head):
        return jnp.dot(
            per_head, spread, precision=lax.Precision.HIGHEST, preferred_element_type=jnp.float32
        )

    summed = sum(gathered[p, :, :acc_width] * widen(rescale[p]) for p in range(pool_size))
    denominator = widen(denominator)
    context = summed / denominator
    attended = context.reshape(tokens_per_device, QUERY_HEADS * HEAD_SIZE).astype(jnp.bfloat16)
    residual = stream.astype(jnp.float32) + jnp.dot(
        attended, output_weight, preferred_element_type=jnp.float32
    )
    meansq = jnp.mean(residual * residual, axis=-1, keepdims=True)
    normed = (residual * lax.rsqrt(meansq + 1e-06) * norm_gain).astype(jnp.bfloat16)
    flat_routes = routes.reshape(-1)
    onehot = (flat_routes[:, None] == jnp.arange(EXPERTS, dtype=jnp.int32)[None, :]).astype(
        jnp.int32
    )
    earlier = jnp.cumsum(onehot, axis=0) - onehot
    slot_of = jnp.sum(earlier * onehot, axis=1)
    destination = flat_routes * CAP + slot_of
    slot_range = jnp.arange(EXPERTS * CAP, dtype=jnp.int32)
    placed = destination.reshape(tokens_per_device, TOPK)[None, :, :] == slot_range[:, None, None]
    send_rows = jnp.dot(
        jnp.any(placed, axis=2).astype(jnp.bfloat16), normed, preferred_element_type=jnp.float32
    ).astype(jnp.bfloat16)
    split = FF // (expert_gate_up.shape[2] // 2)
    expert_rows = direct_dispatch(
        send_rows,
        split,
        jnp.concatenate([expert_gate_up, sibling_gate_up], axis=0),
        jnp.concatenate([expert_down, sibling_down], axis=0),
    )
    mixing = jnp.sum(jnp.where(placed, route_weight[None, :, :], 0.0), axis=2).T
    experts_sum = jnp.dot(
        mixing,
        expert_rows.astype(jnp.float32),
        precision=lax.Precision.HIGHEST,
        preferred_element_type=jnp.float32,
    )
    layer_out = (residual + experts_sum).astype(jnp.bfloat16)
    return (attended, layer_out)


def ring_order(pool_size):
    farthest = pool_size // 2
    return [farthest] + [s for s in range(1, pool_size) if s != farthest] + [0]


def solution(mesh):
    placed = (
        P(("tok", "pool"), None),
        P(("tok", "pool"), None),
        P(("tok", "pool"), None),
        P(("tok", "pool"), None, None),
        P("tok", None),
        P("tok", None),
        P("tok", None),
        P(),
        P(),
        P("tok", None, None),
        P("tok", None, None),
        P(("tok", "pool"), None),
        P(("tok", "pool"), None),
    )
    return jax.shard_map(
        body,
        mesh=mesh,
        in_specs=placed,
        out_specs=(P(("tok", "pool"), None), P(("tok", "pool"), None)),
        check_vma=False,
    )
```

```python
import jax
import jax.numpy as jnp
from jax import lax
from jax.experimental import pallas as pl
from jax.experimental.pallas import tpu as pltpu
from jax.sharding import PartitionSpec as P

QUERY_HEADS = 16
KEY_VALUE_HEADS = 8
HEAD_SIZE = 64
EXPERTS = 32
FF = 512
TOPK = 8
CAP = 32
FRESH_BASE = 1 << 20


score_scale = 0.015625
masked_filler = -1e30


def _attend_kernel(
    source_ref,
    q_ref,
    cache_ref,
    fresh_ref,
    query_len_ref,
    query_seg_ref,
    key_pos_ref,
    key_seg_ref,
    out_ref,
):
    rows = q_ref.shape[0]
    first = pl.multiple_of(source_ref[0] * rows, rows)
    group = query_len_ref.shape[1]
    pick = lax.broadcasted_iota(jnp.int32, (rows, group), 1) == (
        first + lax.broadcasted_iota(jnp.int32, (rows, group), 0)
    )

    def column(row_ref):
        row = row_ref[...].astype(jnp.float32)
        return jnp.sum(jnp.where(pick, row, 0.0), axis=1, keepdims=True).astype(jnp.int32)

    query_len = column(query_len_ref)
    query_seg = column(query_seg_ref)
    query_order = first + lax.broadcasted_iota(jnp.int32, (rows, 1), 0)
    key_pos = key_pos_ref[...]
    shown = (key_pos < query_len) | (
        (key_seg_ref[...] == query_seg) & (key_pos - FRESH_BASE <= query_order)
    )
    lane = lax.broadcasted_iota(jnp.int32, (rows, 128), 1)
    low_half = lane < HEAD_SIZE
    stats = jnp.zeros((rows, 128), jnp.float32)
    heads_per_tile = 128 // HEAD_SIZE
    visible = jnp.concatenate([shown] * (2 * heads_per_tile), axis=0)
    for t in range(KEY_VALUE_HEADS // heads_per_tile):
        v_start = KEY_VALUE_HEADS * HEAD_SIZE + t * 128
        key_tiles = [ref[:, t * 128:(t + 1) * 128] for ref in (cache_ref, fresh_ref)]
        value_tiles = [ref[:, v_start:v_start + 128] for ref in (cache_ref, fresh_ref)]
        pieces = []
        for h in range(t * heads_per_tile, (t + 1) * heads_per_tile):
            q_tile = q_ref[:, h * 128:(h + 1) * 128].astype(jnp.float32)
            for g in range(2):
                q_half = jnp.where(low_half if g == 0 else ~low_half, q_tile, 0.0)
                if g != h % 2:
                    q_half = pltpu.roll(q_half, HEAD_SIZE, 1)
                pieces.append(q_half)
        q_stack = jnp.concatenate(pieces, axis=0).astype(jnp.bfloat16)
        scores = jnp.concatenate(
            [
                lax.dot_general(
                    q_stack, k_tile, (((1,), (1,)), ((), ())), preferred_element_type=jnp.float32
                )
                for k_tile in key_tiles
            ],
            axis=1,
        ) * score_scale
        scores = jnp.where(visible, scores, masked_filler)
        highest = jnp.max(scores, axis=1, keepdims=True)
        weights = jnp.where(visible, jnp.exp(scores - highest), 0.0)
        total = jnp.sum(weights, axis=1, keepdims=True)
        rounded = weights.astype(jnp.bfloat16)
        cached = cache_ref.shape[0]
        acc = jnp.dot(
            rounded[:, :cached], value_tiles[0], preferred_element_type=jnp.float32
        ) + jnp.dot(rounded[:, cached:], value_tiles[1], preferred_element_type=jnp.float32)
        for local, h in enumerate(range(t * heads_per_tile, (t + 1) * heads_per_tile)):
            out_tile = jnp.zeros((rows, 128), jnp.float32)
            for g in range(2):
                at = (2 * local + g) * rows
                part = acc[at:at + rows]
                if g != h % 2:
                    part = pltpu.roll(part, HEAD_SIZE, 1)
                out_tile = jnp.where(low_half if g == 0 else ~low_half, part, out_tile)
                j = 2 * h + g
                stats = jnp.where(lane == j, highest[at:at + rows], stats)
                stats = jnp.where(lane == QUERY_HEADS + j, total[at:at + rows], stats)
            out_ref[:, h * 128:(h + 1) * 128] = out_tile
    out_ref[:, QUERY_HEADS * HEAD_SIZE:QUERY_HEADS * HEAD_SIZE + 128] = stats


def attend_partial(source, q_block, cached, fresh, query_len, query_seg, key_pos, key_seg):
    rows = q_block.shape[0]
    whole = lambda shape: pl.BlockSpec(shape, lambda i, s: (0,) * len(shape))
    operands = (q_block, cached, fresh, query_len, query_seg, key_pos, key_seg)
    return pl.pallas_call(
        _attend_kernel,
        out_shape=jax.ShapeDtypeStruct((rows, QUERY_HEADS * HEAD_SIZE + 128), jnp.float32),
        grid_spec=pltpu.PrefetchScalarGridSpec(
            num_scalar_prefetch=1,
            grid=(1,),
            in_specs=[whole(x.shape) for x in operands],
            out_specs=whole((rows, QUERY_HEADS * HEAD_SIZE + 128)),
        ),
    )(jnp.reshape(source, (1,)).astype(jnp.int32), *operands)


def pair_ffn(rows_in, gate_up_pair, down_pair):
    hidden_units = gate_up_pair.shape[2] // 2
    total = None
    for part in range(gate_up_pair.shape[0]):
        gate_up = jnp.dot(rows_in, gate_up_pair[part], preferred_element_type=jnp.float32)
        inner = (jax.nn.silu(gate_up[:, :hidden_units]) * gate_up[:, hidden_units:]).astype(
            jnp.bfloat16
        )
        produced = jnp.dot(inner, down_pair[part], preferred_element_type=jnp.float32).astype(
            jnp.bfloat16
        ).astype(jnp.float32)
        total = produced if total is None else total + produced
    return total.astype(jnp.bfloat16)


def direct_dispatch(send_rows, split, expert_gate_up, expert_down):
    width = send_rows.shape[1]
    gate_up_pair, down_pair = expert_gate_up, expert_down
    unit_rows = send_rows.reshape(EXPERTS * split, CAP // split, width)
    arrived = lax.all_to_all(unit_rows, "tok", split_axis=0, concat_axis=0, tiled=True)
    produced = pair_ffn(arrived.reshape(-1, width), gate_up_pair, down_pair)
    returned = lax.all_to_all(
        produced.reshape(EXPERTS * split, CAP // split, width),
        "tok",
        split_axis=0,
        concat_axis=0,
        tiled=True,
    )
    return returned.reshape(EXPERTS * CAP, width)


def body(
    stream,
    queries,
    fresh_kv,
    cache_block_pool,
    block_table,
    cached_len,
    request_ids,
    output_weight,
    norm_gain,
    expert_gate_up,
    expert_down,
    routes,
    route_weight,
):
    tokens_per_device = stream.shape[0]
    tok_size = lax.axis_size("tok")
    sibling = [(t, t ^ 1) for t in range(tok_size)]
    sibling_gate_up = lax.ppermute(expert_gate_up, "tok", sibling)
    sibling_down = lax.ppermute(expert_down, "tok", sibling)
    kv_width = KEY_VALUE_HEADS * HEAD_SIZE
    pool_size = lax.axis_size("pool")
    pool_idx = lax.axis_index("pool")
    segments = request_ids[0]
    lengths = cached_len[0]
    table = block_table[0]
    list_len = table.shape[0]
    pool_blocks = cache_block_pool.shape[0]
    block_len = cache_block_pool.shape[1]
    request_range = jnp.arange(lengths.shape[0], dtype=jnp.int32)
    row_len = jnp.sum(
        jnp.where(segments[:, None] == request_range[None, :], lengths[None, :], 0), axis=1
    )
    local_slots = pool_idx * pool_blocks + jnp.arange(pool_blocks, dtype=jnp.int32)
    slot_block = (
        jnp.sum(
            jnp.where(
                table[None, :] == local_slots[:, None],
                jnp.arange(list_len, dtype=jnp.int32)[None, :] + 1,
                0,
            ),
            axis=1,
        )
        - 1
    )
    offsets = jnp.arange(block_len, dtype=jnp.int32)
    cache_pos = (slot_block[:, None] * block_len + offsets[None, :]).reshape(-1)
    cache_listed = jnp.repeat(slot_block >= 0, block_len)
    shifts = range(pool_size)
    fresh_order = pool_idx * tokens_per_device + jnp.arange(tokens_per_device, dtype=jnp.int32)
    fresh_seg = lax.dynamic_slice_in_dim(segments, pool_idx * tokens_per_device, tokens_per_device)
    cached_rows = cache_block_pool.reshape(pool_blocks * block_len, 2 * kv_width)

    unlisted = jnp.int32(1 << 30)
    key_pos = jnp.concatenate(
        [jnp.where(cache_listed, cache_pos, unlisted), FRESH_BASE + fresh_order]
    ).reshape(1, -1)
    key_seg = jnp.concatenate(
        [jnp.full((pool_blocks * block_len,), -1, jnp.int32), fresh_seg]
    ).reshape(1, -1)
    query_len_all = jnp.sum(
        jnp.where(
            request_ids[:, :, None] == request_range[None, None, :], lengths[None, None, :], 0
        ),
        axis=2,
    )
    query_seg_all = request_ids

    def attend_block(query_block, source):
        return attend_partial(
            source,
            query_block,
            cached_rows,
            fresh_kv,
            query_len_all,
            query_seg_all,
            key_pos,
            key_seg,
        )

    query_blocks = [queries] + [
        lax.ppermute(
            queries, "pool", [(i, (i + shift) % pool_size) for i in range(pool_size)]
        )
        for shift in shifts[1:]
    ]
    partials = [None] * pool_size
    for shift in ring_order(pool_size):
        partial = attend_block(query_blocks[shift], (pool_idx - shift) % pool_size)
        if shift:
            partial = lax.ppermute(
                partial, "pool", [(i, (i - shift) % pool_size) for i in range(pool_size)]
            )
        partials[shift] = partial
    gathered = jnp.stack(partials)
    acc_width = QUERY_HEADS * HEAD_SIZE
    part_max = gathered[:, :, acc_width : acc_width + QUERY_HEADS]
    part_sum = gathered[:, :, acc_width + QUERY_HEADS : acc_width + 2 * QUERY_HEADS]
    running = jnp.max(part_max, axis=0)
    rescale = jnp.exp(part_max - running[None])
    denominator = jnp.sum(part_sum * rescale, axis=0)
    spread = (
        jnp.arange(acc_width, dtype=jnp.int32)[None, :] // HEAD_SIZE
        == jnp.arange(QUERY_HEADS, dtype=jnp.int32)[:, None]
    ).astype(jnp.float32)

    def widen(per_head):
        return jnp.dot(
            per_head, spread, precision=lax.Precision.HIGHEST, preferred_element_type=jnp.float32
        )

    summed = sum(gathered[p, :, :acc_width] * widen(rescale[p]) for p in range(pool_size))
    denominator = widen(denominator)
    context = summed / denominator
    attended = context.reshape(tokens_per_device, QUERY_HEADS * HEAD_SIZE).astype(jnp.bfloat16)
    residual = stream.astype(jnp.float32) + jnp.dot(
        attended, output_weight, preferred_element_type=jnp.float32
    )
    meansq = jnp.mean(residual * residual, axis=-1, keepdims=True)
    normed = (residual * lax.rsqrt(meansq + 1e-06) * norm_gain).astype(jnp.bfloat16)
    flat_routes = routes.reshape(-1)
    onehot = (flat_routes[:, None] == jnp.arange(EXPERTS, dtype=jnp.int32)[None, :]).astype(
        jnp.int32
    )
    earlier = jnp.cumsum(onehot, axis=0) - onehot
    slot_of = jnp.sum(earlier * onehot, axis=1)
    destination = flat_routes * CAP + slot_of
    slot_range = jnp.arange(EXPERTS * CAP, dtype=jnp.int32)
    placed = destination.reshape(tokens_per_device, TOPK)[None, :, :] == slot_range[:, None, None]
    send_rows = jnp.dot(
        jnp.any(placed, axis=2).astype(jnp.bfloat16), normed, preferred_element_type=jnp.float32
    ).astype(jnp.bfloat16)
    split = FF // (expert_gate_up.shape[2] // 2)
    expert_rows = direct_dispatch(
        send_rows,
        split,
        jnp.concatenate([expert_gate_up, sibling_gate_up], axis=0),
        jnp.concatenate([expert_down, sibling_down], axis=0),
    )
    mixing = jnp.sum(jnp.where(placed, route_weight[None, :, :], 0.0), axis=2).T
    experts_sum = jnp.dot(
        mixing,
        expert_rows.astype(jnp.float32),
        precision=lax.Precision.HIGH,
        preferred_element_type=jnp.float32,
    )
    layer_out = (residual + experts_sum).astype(jnp.bfloat16)
    return (attended, layer_out)


def ring_order(pool_size):
    farthest = pool_size // 2
    return [farthest] + [s for s in range(1, pool_size) if s != farthest] + [0]


def solution(mesh):
    placed = (
        P(("tok", "pool"), None),
        P(("tok", "pool"), None),
        P(("tok", "pool"), None),
        P(("tok", "pool"), None, None),
        P("tok", None),
        P("tok", None),
        P("tok", None),
        P(),
        P(),
        P("tok", None, None),
        P("tok", None, None),
        P(("tok", "pool"), None),
        P(("tok", "pool"), None),
    )
    return jax.shard_map(
        body,
        mesh=mesh,
        in_specs=placed,
        out_specs=(P(("tok", "pool"), None), P(("tok", "pool"), None)),
        check_vma=False,
    )
```

```python
import jax
import jax.numpy as jnp
from jax import lax
from jax.experimental import pallas as pl
from jax.experimental.pallas import tpu as pltpu
from jax.sharding import PartitionSpec as P

QUERY_HEADS = 16
KEY_VALUE_HEADS = 8
HEAD_SIZE = 64
EXPERTS = 32
FF = 512
TOPK = 8
CAP = 32
FRESH_BASE = 1 << 20


score_scale = 0.015625
masked_filler = -1e30


def _attend_kernel(
    source_ref,
    q_ref,
    cache_ref,
    fresh_ref,
    query_len_ref,
    query_seg_ref,
    key_pos_ref,
    key_seg_ref,
    out_ref,
):
    rows = q_ref.shape[0]
    first = pl.multiple_of(source_ref[0] * rows, rows)
    group = query_len_ref.shape[1]
    pick = lax.broadcasted_iota(jnp.int32, (rows, group), 1) == (
        first + lax.broadcasted_iota(jnp.int32, (rows, group), 0)
    )

    def column(row_ref):
        row = row_ref[...].astype(jnp.float32)
        return jnp.sum(jnp.where(pick, row, 0.0), axis=1, keepdims=True).astype(jnp.int32)

    query_len = column(query_len_ref)
    query_seg = column(query_seg_ref)
    query_order = first + lax.broadcasted_iota(jnp.int32, (rows, 1), 0)
    key_pos = key_pos_ref[...]
    shown = (key_pos < query_len) | (
        (key_seg_ref[...] == query_seg) & (key_pos - FRESH_BASE <= query_order)
    )
    lane = lax.broadcasted_iota(jnp.int32, (rows, 128), 1)
    low_half = lane < HEAD_SIZE
    stats = jnp.zeros((rows, 128), jnp.float32)
    heads_per_tile = 128 // HEAD_SIZE
    visible = jnp.concatenate([shown] * (2 * heads_per_tile), axis=0)
    for t in range(KEY_VALUE_HEADS // heads_per_tile):
        v_start = KEY_VALUE_HEADS * HEAD_SIZE + t * 128
        key_tiles = [ref[:, t * 128:(t + 1) * 128] for ref in (cache_ref, fresh_ref)]
        value_tiles = [ref[:, v_start:v_start + 128] for ref in (cache_ref, fresh_ref)]
        pieces = []
        for h in range(t * heads_per_tile, (t + 1) * heads_per_tile):
            q_tile = q_ref[:, h * 128:(h + 1) * 128].astype(jnp.float32)
            for g in range(2):
                q_half = jnp.where(low_half if g == 0 else ~low_half, q_tile, 0.0)
                if g != h % 2:
                    q_half = pltpu.roll(q_half, HEAD_SIZE, 1)
                pieces.append(q_half)
        q_stack = jnp.concatenate(pieces, axis=0).astype(jnp.bfloat16)
        scores = jnp.concatenate(
            [
                lax.dot_general(
                    q_stack, k_tile, (((1,), (1,)), ((), ())), preferred_element_type=jnp.float32
                )
                for k_tile in key_tiles
            ],
            axis=1,
        ) * score_scale
        scores = jnp.where(visible, scores, masked_filler)
        highest = jnp.max(scores, axis=1, keepdims=True)
        weights = jnp.where(visible, jnp.exp(scores - highest), 0.0)
        total = jnp.sum(weights, axis=1, keepdims=True)
        rounded = weights.astype(jnp.bfloat16)
        cached = cache_ref.shape[0]
        acc = jnp.dot(
            rounded[:, :cached], value_tiles[0], preferred_element_type=jnp.float32
        ) + jnp.dot(rounded[:, cached:], value_tiles[1], preferred_element_type=jnp.float32)
        for local, h in enumerate(range(t * heads_per_tile, (t + 1) * heads_per_tile)):
            out_tile = jnp.zeros((rows, 128), jnp.float32)
            for g in range(2):
                at = (2 * local + g) * rows
                part = acc[at:at + rows]
                if g != h % 2:
                    part = pltpu.roll(part, HEAD_SIZE, 1)
                out_tile = jnp.where(low_half if g == 0 else ~low_half, part, out_tile)
                j = 2 * h + g
                stats = jnp.where(lane == j, highest[at:at + rows], stats)
                stats = jnp.where(lane == QUERY_HEADS + j, total[at:at + rows], stats)
            out_ref[:, h * 128:(h + 1) * 128] = out_tile
    out_ref[:, QUERY_HEADS * HEAD_SIZE:QUERY_HEADS * HEAD_SIZE + 128] = stats


def attend_partial(source, q_block, cached, fresh, query_len, query_seg, key_pos, key_seg):
    rows = q_block.shape[0]
    whole = lambda shape: pl.BlockSpec(shape, lambda i, s: (0,) * len(shape))
    operands = (q_block, cached, fresh, query_len, query_seg, key_pos, key_seg)
    return pl.pallas_call(
        _attend_kernel,
        out_shape=jax.ShapeDtypeStruct((rows, QUERY_HEADS * HEAD_SIZE + 128), jnp.float32),
        grid_spec=pltpu.PrefetchScalarGridSpec(
            num_scalar_prefetch=1,
            grid=(1,),
            in_specs=[whole(x.shape) for x in operands],
            out_specs=whole((rows, QUERY_HEADS * HEAD_SIZE + 128)),
        ),
    )(jnp.reshape(source, (1,)).astype(jnp.int32), *operands)


def pair_ffn(rows_in, gate_up_pair, down_pair):
    parts = gate_up_pair.shape[0]
    hidden_units = gate_up_pair.shape[2] // 2
    joined = jnp.concatenate([gate_up_pair[part] for part in range(parts)], axis=1)
    gate_up_all = jnp.dot(rows_in, joined, preferred_element_type=jnp.float32)
    total = None
    for part in range(parts):
        gate_up = gate_up_all[:, part * 2 * hidden_units:(part + 1) * 2 * hidden_units]
        inner = (jax.nn.silu(gate_up[:, :hidden_units]) * gate_up[:, hidden_units:]).astype(
            jnp.bfloat16
        )
        produced = jnp.dot(inner, down_pair[part], preferred_element_type=jnp.float32).astype(
            jnp.bfloat16
        ).astype(jnp.float32)
        total = produced if total is None else total + produced
    return total.astype(jnp.bfloat16)


def direct_dispatch(send_rows, split, expert_gate_up, expert_down):
    width = send_rows.shape[1]
    gate_up_pair, down_pair = expert_gate_up, expert_down
    unit_rows = send_rows.reshape(EXPERTS * split, CAP // split, width)
    arrived = lax.all_to_all(unit_rows, "tok", split_axis=0, concat_axis=0, tiled=True)
    produced = pair_ffn(arrived.reshape(-1, width), gate_up_pair, down_pair)
    returned = lax.all_to_all(
        produced.reshape(EXPERTS * split, CAP // split, width),
        "tok",
        split_axis=0,
        concat_axis=0,
        tiled=True,
    )
    return returned.reshape(EXPERTS * CAP, width)


def body(
    stream,
    queries,
    fresh_kv,
    cache_block_pool,
    block_table,
    cached_len,
    request_ids,
    output_weight,
    norm_gain,
    expert_gate_up,
    expert_down,
    routes,
    route_weight,
):
    tokens_per_device = stream.shape[0]
    tok_size = lax.axis_size("tok")
    sibling = [(t, t ^ 1) for t in range(tok_size)]
    sibling_gate_up = lax.ppermute(expert_gate_up, "tok", sibling)
    sibling_down = lax.ppermute(expert_down, "tok", sibling)
    kv_width = KEY_VALUE_HEADS * HEAD_SIZE
    pool_size = lax.axis_size("pool")
    pool_idx = lax.axis_index("pool")
    segments = request_ids[0]
    lengths = cached_len[0]
    table = block_table[0]
    list_len = table.shape[0]
    pool_blocks = cache_block_pool.shape[0]
    block_len = cache_block_pool.shape[1]
    request_range = jnp.arange(lengths.shape[0], dtype=jnp.int32)
    row_len = jnp.sum(
        jnp.where(segments[:, None] == request_range[None, :], lengths[None, :], 0), axis=1
    )
    local_slots = pool_idx * pool_blocks + jnp.arange(pool_blocks, dtype=jnp.int32)
    slot_block = (
        jnp.sum(
            jnp.where(
                table[None, :] == local_slots[:, None],
                jnp.arange(list_len, dtype=jnp.int32)[None, :] + 1,
                0,
            ),
            axis=1,
        )
        - 1
    )
    offsets = jnp.arange(block_len, dtype=jnp.int32)
    cache_pos = (slot_block[:, None] * block_len + offsets[None, :]).reshape(-1)
    cache_listed = jnp.repeat(slot_block >= 0, block_len)
    shifts = range(pool_size)
    fresh_order = pool_idx * tokens_per_device + jnp.arange(tokens_per_device, dtype=jnp.int32)
    fresh_seg = lax.dynamic_slice_in_dim(segments, pool_idx * tokens_per_device, tokens_per_device)
    cached_rows = cache_block_pool.reshape(pool_blocks * block_len, 2 * kv_width)

    unlisted = jnp.int32(1 << 30)
    key_pos = jnp.concatenate(
        [jnp.where(cache_listed, cache_pos, unlisted), FRESH_BASE + fresh_order]
    ).reshape(1, -1)
    key_seg = jnp.concatenate(
        [jnp.full((pool_blocks * block_len,), -1, jnp.int32), fresh_seg]
    ).reshape(1, -1)
    query_len_all = jnp.sum(
        jnp.where(
            request_ids[:, :, None] == request_range[None, None, :], lengths[None, None, :], 0
        ),
        axis=2,
    )
    query_seg_all = request_ids

    def attend_block(query_block, source):
        return attend_partial(
            source,
            query_block,
            cached_rows,
            fresh_kv,
            query_len_all,
            query_seg_all,
            key_pos,
            key_seg,
        )

    query_blocks = [queries] + [
        lax.ppermute(
            queries, "pool", [(i, (i + shift) % pool_size) for i in range(pool_size)]
        )
        for shift in shifts[1:]
    ]
    partials = [None] * pool_size
    for shift in ring_order(pool_size):
        partial = attend_block(query_blocks[shift], (pool_idx - shift) % pool_size)
        if shift:
            partial = lax.ppermute(
                partial, "pool", [(i, (i - shift) % pool_size) for i in range(pool_size)]
            )
        partials[shift] = partial
    gathered = jnp.stack(partials)
    acc_width = QUERY_HEADS * HEAD_SIZE
    part_max = gathered[:, :, acc_width : acc_width + QUERY_HEADS]
    part_sum = gathered[:, :, acc_width + QUERY_HEADS : acc_width + 2 * QUERY_HEADS]
    running = jnp.max(part_max, axis=0)
    rescale = jnp.exp(part_max - running[None])
    denominator = jnp.sum(part_sum * rescale, axis=0)
    spread = (
        jnp.arange(acc_width, dtype=jnp.int32)[None, :] // HEAD_SIZE
        == jnp.arange(QUERY_HEADS, dtype=jnp.int32)[:, None]
    ).astype(jnp.float32)

    def widen(per_head):
        return jnp.dot(
            per_head, spread, precision=lax.Precision.HIGHEST, preferred_element_type=jnp.float32
        )

    summed = sum(gathered[p, :, :acc_width] * widen(rescale[p]) for p in range(pool_size))
    denominator = widen(denominator)
    context = summed / denominator
    attended = context.reshape(tokens_per_device, QUERY_HEADS * HEAD_SIZE).astype(jnp.bfloat16)
    residual = stream.astype(jnp.float32) + jnp.dot(
        attended, output_weight, preferred_element_type=jnp.float32
    )
    meansq = jnp.mean(residual * residual, axis=-1, keepdims=True)
    normed = (residual * lax.rsqrt(meansq + 1e-06) * norm_gain).astype(jnp.bfloat16)
    flat_routes = routes.reshape(-1)
    onehot = (flat_routes[:, None] == jnp.arange(EXPERTS, dtype=jnp.int32)[None, :]).astype(
        jnp.int32
    )
    earlier = jnp.cumsum(onehot, axis=0) - onehot
    slot_of = jnp.sum(earlier * onehot, axis=1)
    destination = flat_routes * CAP + slot_of
    slot_range = jnp.arange(EXPERTS * CAP, dtype=jnp.int32)
    placed = destination.reshape(tokens_per_device, TOPK)[None, :, :] == slot_range[:, None, None]
    send_rows = jnp.dot(
        jnp.any(placed, axis=2).astype(jnp.bfloat16), normed, preferred_element_type=jnp.float32
    ).astype(jnp.bfloat16)
    split = FF // (expert_gate_up.shape[2] // 2)
    expert_rows = direct_dispatch(
        send_rows,
        split,
        jnp.concatenate([expert_gate_up, sibling_gate_up], axis=0),
        jnp.concatenate([expert_down, sibling_down], axis=0),
    )
    mixing = jnp.sum(jnp.where(placed, route_weight[None, :, :], 0.0), axis=2).T
    experts_sum = jnp.dot(
        mixing,
        expert_rows.astype(jnp.float32),
        precision=lax.Precision.HIGHEST,
        preferred_element_type=jnp.float32,
    )
    layer_out = (residual + experts_sum).astype(jnp.bfloat16)
    return (attended, layer_out)


def ring_order(pool_size):
    farthest = pool_size // 2
    return [farthest] + [s for s in range(1, pool_size) if s != farthest] + [0]


def solution(mesh):
    placed = (
        P(("tok", "pool"), None),
        P(("tok", "pool"), None),
        P(("tok", "pool"), None),
        P(("tok", "pool"), None, None),
        P("tok", None),
        P("tok", None),
        P("tok", None),
        P(),
        P(),
        P("tok", None, None),
        P("tok", None, None),
        P(("tok", "pool"), None),
        P(("tok", "pool"), None),
    )
    return jax.shard_map(
        body,
        mesh=mesh,
        in_specs=placed,
        out_specs=(P(("tok", "pool"), None), P(("tok", "pool"), None)),
        check_vma=False,
    )
```

```python
import jax
import jax.numpy as jnp
from jax import lax
from jax.experimental import pallas as pl
from jax.experimental.pallas import tpu as pltpu
from jax.sharding import PartitionSpec as P

QUERY_HEADS = 16
KEY_VALUE_HEADS = 8
HEAD_SIZE = 64
EXPERTS = 32
FF = 512
TOPK = 8
CAP = 32
FRESH_BASE = 1 << 20


score_scale = 0.015625
masked_filler = -1e30


def _attend_kernel(
    source_ref,
    q_ref,
    cache_ref,
    fresh_ref,
    query_len_ref,
    query_seg_ref,
    key_info_ref,
    out_ref,
):
    rows = q_ref.shape[0]
    first = pl.multiple_of(source_ref[0] * rows, rows)
    group = query_len_ref.shape[1]
    pick = lax.broadcasted_iota(jnp.int32, (rows, group), 1) == (
        first + lax.broadcasted_iota(jnp.int32, (rows, group), 0)
    )

    def column(row_ref):
        row = row_ref[...].astype(jnp.float32)
        return jnp.sum(jnp.where(pick, row, 0.0), axis=1, keepdims=True).astype(jnp.int32)

    query_len = column(query_len_ref)
    query_seg = column(query_seg_ref)
    query_order = first + lax.broadcasted_iota(jnp.int32, (rows, 1), 0)
    key_pos = key_info_ref[0:1, :]
    shown = (key_pos < query_len) | (
        (key_info_ref[1:2, :] == query_seg) & (key_pos - FRESH_BASE <= query_order)
    )
    lane = lax.broadcasted_iota(jnp.int32, (rows, 128), 1)
    low_half = lane < HEAD_SIZE
    stats = jnp.zeros((rows, 128), jnp.float32)
    heads_per_tile = 128 // HEAD_SIZE
    visible = jnp.concatenate([shown] * (2 * heads_per_tile), axis=0)
    for t in range(KEY_VALUE_HEADS // heads_per_tile):
        v_start = KEY_VALUE_HEADS * HEAD_SIZE + t * 128
        key_tiles = [ref[:, t * 128:(t + 1) * 128] for ref in (cache_ref, fresh_ref)]
        value_tiles = [ref[:, v_start:v_start + 128] for ref in (cache_ref, fresh_ref)]
        pieces = []
        for h in range(t * heads_per_tile, (t + 1) * heads_per_tile):
            q_tile = q_ref[:, h * 128:(h + 1) * 128].astype(jnp.float32)
            for g in range(2):
                q_half = jnp.where(low_half if g == 0 else ~low_half, q_tile, 0.0)
                if g != h % 2:
                    q_half = pltpu.roll(q_half, HEAD_SIZE, 1)
                pieces.append(q_half)
        q_stack = jnp.concatenate(pieces, axis=0).astype(jnp.bfloat16)
        scores = jnp.concatenate(
            [
                lax.dot_general(
                    q_stack, k_tile, (((1,), (1,)), ((), ())), preferred_element_type=jnp.float32
                )
                for k_tile in key_tiles
            ],
            axis=1,
        ) * score_scale
        scores = jnp.where(visible, scores, masked_filler)
        highest = jnp.max(scores, axis=1, keepdims=True)
        weights = jnp.where(visible, jnp.exp(scores - highest), 0.0)
        total = jnp.sum(weights, axis=1, keepdims=True)
        rounded = weights.astype(jnp.bfloat16)
        cached = cache_ref.shape[0]
        acc = jnp.dot(
            rounded[:, :cached], value_tiles[0], preferred_element_type=jnp.float32
        ) + jnp.dot(rounded[:, cached:], value_tiles[1], preferred_element_type=jnp.float32)
        for local, h in enumerate(range(t * heads_per_tile, (t + 1) * heads_per_tile)):
            out_tile = jnp.zeros((rows, 128), jnp.float32)
            for g in range(2):
                at = (2 * local + g) * rows
                part = acc[at:at + rows]
                if g != h % 2:
                    part = pltpu.roll(part, HEAD_SIZE, 1)
                out_tile = jnp.where(low_half if g == 0 else ~low_half, part, out_tile)
                j = 2 * h + g
                stats = jnp.where(lane == j, highest[at:at + rows], stats)
                stats = jnp.where(lane == QUERY_HEADS + j, total[at:at + rows], stats)
            out_ref[:, h * 128:(h + 1) * 128] = out_tile
    out_ref[:, QUERY_HEADS * HEAD_SIZE:QUERY_HEADS * HEAD_SIZE + 128] = stats


def attend_partial(source, q_block, cached, fresh, query_len, query_seg, key_info):
    rows = q_block.shape[0]
    whole = lambda shape: pl.BlockSpec(shape, lambda i, s: (0,) * len(shape))
    operands = (q_block, cached, fresh, query_len, query_seg, key_info)
    return pl.pallas_call(
        _attend_kernel,
        out_shape=jax.ShapeDtypeStruct((rows, QUERY_HEADS * HEAD_SIZE + 128), jnp.float32),
        grid_spec=pltpu.PrefetchScalarGridSpec(
            num_scalar_prefetch=1,
            grid=(1,),
            in_specs=[whole(x.shape) for x in operands],
            out_specs=whole((rows, QUERY_HEADS * HEAD_SIZE + 128)),
        ),
    )(jnp.reshape(source, (1,)).astype(jnp.int32), *operands)


def pair_ffn(rows_in, gate_up_pair, down_pair):
    hidden_units = gate_up_pair.shape[2] // 2
    total = None
    for part in range(gate_up_pair.shape[0]):
        gate_up = jnp.dot(rows_in, gate_up_pair[part], preferred_element_type=jnp.float32)
        inner = (jax.nn.silu(gate_up[:, :hidden_units]) * gate_up[:, hidden_units:]).astype(
            jnp.bfloat16
        )
        produced = jnp.dot(inner, down_pair[part], preferred_element_type=jnp.float32).astype(
            jnp.bfloat16
        ).astype(jnp.float32)
        total = produced if total is None else total + produced
    return total.astype(jnp.bfloat16)


def direct_dispatch(send_rows, split, expert_gate_up, expert_down):
    width = send_rows.shape[1]
    gate_up_pair, down_pair = expert_gate_up, expert_down
    unit_rows = send_rows.reshape(EXPERTS * split, CAP // split, width)
    arrived = lax.all_to_all(unit_rows, "tok", split_axis=0, concat_axis=0, tiled=True)
    produced = pair_ffn(arrived.reshape(-1, width), gate_up_pair, down_pair)
    returned = lax.all_to_all(
        produced.reshape(EXPERTS * split, CAP // split, width),
        "tok",
        split_axis=0,
        concat_axis=0,
        tiled=True,
    )
    return returned.reshape(EXPERTS * CAP, width)


def body(
    stream,
    queries,
    fresh_kv,
    cache_block_pool,
    block_table,
    cached_len,
    request_ids,
    output_weight,
    norm_gain,
    expert_gate_up,
    expert_down,
    routes,
    route_weight,
):
    tokens_per_device = stream.shape[0]
    tok_size = lax.axis_size("tok")
    sibling = [(t, t ^ 1) for t in range(tok_size)]
    sibling_gate_up = lax.ppermute(expert_gate_up, "tok", sibling)
    sibling_down = lax.ppermute(expert_down, "tok", sibling)
    kv_width = KEY_VALUE_HEADS * HEAD_SIZE
    pool_size = lax.axis_size("pool")
    pool_idx = lax.axis_index("pool")
    segments = request_ids[0]
    lengths = cached_len[0]
    table = block_table[0]
    list_len = table.shape[0]
    pool_blocks = cache_block_pool.shape[0]
    block_len = cache_block_pool.shape[1]
    request_range = jnp.arange(lengths.shape[0], dtype=jnp.int32)
    row_len = jnp.sum(
        jnp.where(segments[:, None] == request_range[None, :], lengths[None, :], 0), axis=1
    )
    local_slots = pool_idx * pool_blocks + jnp.arange(pool_blocks, dtype=jnp.int32)
    slot_block = (
        jnp.sum(
            jnp.where(
                table[None, :] == local_slots[:, None],
                jnp.arange(list_len, dtype=jnp.int32)[None, :] + 1,
                0,
            ),
            axis=1,
        )
        - 1
    )
    offsets = jnp.arange(block_len, dtype=jnp.int32)
    cache_pos = (slot_block[:, None] * block_len + offsets[None, :]).reshape(-1)
    cache_listed = jnp.repeat(slot_block >= 0, block_len)
    shifts = range(pool_size)
    fresh_order = pool_idx * tokens_per_device + jnp.arange(tokens_per_device, dtype=jnp.int32)
    fresh_seg = lax.dynamic_slice_in_dim(segments, pool_idx * tokens_per_device, tokens_per_device)
    cached_rows = cache_block_pool.reshape(pool_blocks * block_len, 2 * kv_width)

    unlisted = jnp.int32(1 << 30)
    key_info = jnp.stack(
        [
            jnp.concatenate(
                [jnp.where(cache_listed, cache_pos, unlisted), FRESH_BASE + fresh_order]
            ),
            jnp.concatenate([jnp.full((pool_blocks * block_len,), -1, jnp.int32), fresh_seg]),
        ]
    )
    query_len_all = jnp.sum(
        jnp.where(
            request_ids[:, :, None] == request_range[None, None, :], lengths[None, None, :], 0
        ),
        axis=2,
    )
    query_seg_all = request_ids

    def attend_block(query_block, source):
        return attend_partial(
            source,
            query_block,
            cached_rows,
            fresh_kv,
            query_len_all,
            query_seg_all,
            key_info,
        )

    query_blocks = [queries] + [
        lax.ppermute(
            queries, "pool", [(i, (i + shift) % pool_size) for i in range(pool_size)]
        )
        for shift in shifts[1:]
    ]
    partials = [None] * pool_size
    for shift in ring_order(pool_size):
        partial = attend_block(query_blocks[shift], (pool_idx - shift) % pool_size)
        if shift:
            partial = lax.ppermute(
                partial, "pool", [(i, (i - shift) % pool_size) for i in range(pool_size)]
            )
        partials[shift] = partial
    gathered = jnp.stack(partials)
    acc_width = QUERY_HEADS * HEAD_SIZE
    part_max = gathered[:, :, acc_width : acc_width + QUERY_HEADS]
    part_sum = gathered[:, :, acc_width + QUERY_HEADS : acc_width + 2 * QUERY_HEADS]
    running = jnp.max(part_max, axis=0)
    rescale = jnp.exp(part_max - running[None])
    denominator = jnp.sum(part_sum * rescale, axis=0)
    spread = (
        jnp.arange(acc_width, dtype=jnp.int32)[None, :] // HEAD_SIZE
        == jnp.arange(QUERY_HEADS, dtype=jnp.int32)[:, None]
    ).astype(jnp.float32)

    def widen(per_head):
        return jnp.dot(
            per_head, spread, precision=lax.Precision.HIGHEST, preferred_element_type=jnp.float32
        )

    summed = sum(gathered[p, :, :acc_width] * widen(rescale[p]) for p in range(pool_size))
    denominator = widen(denominator)
    context = summed / denominator
    attended = context.reshape(tokens_per_device, QUERY_HEADS * HEAD_SIZE).astype(jnp.bfloat16)
    residual = stream.astype(jnp.float32) + jnp.dot(
        attended, output_weight, preferred_element_type=jnp.float32
    )
    meansq = jnp.mean(residual * residual, axis=-1, keepdims=True)
    normed = (residual * lax.rsqrt(meansq + 1e-06) * norm_gain).astype(jnp.bfloat16)
    flat_routes = routes.reshape(-1)
    onehot = (flat_routes[:, None] == jnp.arange(EXPERTS, dtype=jnp.int32)[None, :]).astype(
        jnp.int32
    )
    earlier = jnp.cumsum(onehot, axis=0) - onehot
    slot_of = jnp.sum(earlier * onehot, axis=1)
    destination = flat_routes * CAP + slot_of
    slot_range = jnp.arange(EXPERTS * CAP, dtype=jnp.int32)
    placed = destination.reshape(tokens_per_device, TOPK)[None, :, :] == slot_range[:, None, None]
    send_rows = jnp.dot(
        jnp.any(placed, axis=2).astype(jnp.bfloat16), normed, preferred_element_type=jnp.float32
    ).astype(jnp.bfloat16)
    split = FF // (expert_gate_up.shape[2] // 2)
    expert_rows = direct_dispatch(
        send_rows,
        split,
        jnp.concatenate([expert_gate_up, sibling_gate_up], axis=0),
        jnp.concatenate([expert_down, sibling_down], axis=0),
    )
    mixing = jnp.sum(jnp.where(placed, route_weight[None, :, :], 0.0), axis=2).T
    experts_sum = jnp.dot(
        mixing,
        expert_rows.astype(jnp.float32),
        precision=lax.Precision.HIGHEST,
        preferred_element_type=jnp.float32,
    )
    layer_out = (residual + experts_sum).astype(jnp.bfloat16)
    return (attended, layer_out)


def ring_order(pool_size):
    farthest = pool_size // 2
    return [farthest] + [s for s in range(1, pool_size) if s != farthest] + [0]


def solution(mesh):
    placed = (
        P(("tok", "pool"), None),
        P(("tok", "pool"), None),
        P(("tok", "pool"), None),
        P(("tok", "pool"), None, None),
        P("tok", None),
        P("tok", None),
        P("tok", None),
        P(),
        P(),
        P("tok", None, None),
        P("tok", None, None),
        P(("tok", "pool"), None),
        P(("tok", "pool"), None),
    )
    return jax.shard_map(
        body,
        mesh=mesh,
        in_specs=placed,
        out_specs=(P(("tok", "pool"), None), P(("tok", "pool"), None)),
        check_vma=False,
    )
```
